512 devices in a mesh: depth: 16 (over z_lo, x, core), height: 8 (over y), sample: 4 (over z_hi).
Axes of the slice: x: 4, y: 8, z: 8 (z_hi: 4, z_lo: 2; z = z_hi * 2 + z_lo), core: 2. Of those that a mesh axis runs over, the one named last changes fastest.
Arguments:
- volume: bfloat16 [4, 4, 64, 32, 512], P('sample', None, 'depth', 'height'), may hold values from -6 to 6
- kernel_one: bfloat16 [32, 108], replicated, may hold values from -0.625 to 0.625
- kernel_two: bfloat16 [64, 864], P('height'), may hold values from -0.21875 to 0.21875
- cotangent: bfloat16 [4, 64, 16, 1024], P('sample', 'height', 'depth'), may hold values from -24 to 24
Outputs:
- pooled_two: bfloat16 [4, 64, 16, 1024], P('sample', 'height', 'depth')
- weight_grad: float32 [64, 864], P('height')
- act_grad: bfloat16 [4, 32, 32, 16, 256], P('sample', None, 'depth', 'height')
The draws below stay inside these ranges and needn't reach their ends.
All inputs are finite; a program needn't handle non-finite values.
Results may differ from the reference program's by a relative error of at most 0.005.
Values may be sent and summed in bfloat16 or wider, within the bound.
No kernel may reach another device: no remote copies, remote signals or barrier semaphores. Data moves between devices by JAX's collectives and lax.ppermute only.
A program may use at most 64 MiB of HBM per device.

```python
import jax
import jax.numpy as jnp
from jax import lax

C0 = 4
C1 = 32
C2 = 64
WIDTH = 512
SAMPLES = 4
DEPTH = 64
HEIGHT = 32


def level_of(rng, extent, pieces, least, largest):
    def one(dim, blocks):
        steps = jax.random.uniform(jax.random.fold_in(jax.random.fold_in(rng, 6), dim), (blocks,), jnp.float32, least / len(pieces), largest / len(pieces))
        return jnp.repeat(jnp.exp(steps), extent[dim] // blocks).reshape((-1,) + (1,) * (len(extent) - dim - 1))

    gain = one(*pieces[0])
    for cut in pieces[1:]:
        gain = gain * one(*cut)
    return gain


def normal_values(own_key, extent, width, bound, pieces=(), held_as=jnp.bfloat16):
    gain = level_of(own_key, extent, pieces, -0.22, 0.18) if pieces else 1.0
    entries = jax.random.normal(own_key, extent, jnp.float32) * width * gain
    return jnp.minimum(jnp.maximum(entries, -bound), bound).astype(held_as)


def setup_inputs(seed: int = 0) -> dict:
    keys = jax.random.split(jax.random.key(seed), 5)
    return {
        "volume": normal_values(keys[0], (SAMPLES, C0, DEPTH, HEIGHT, WIDTH), 1.0, 6.0, ((0, 4), (2, 16), (3, 8))),
        "kernel_one": normal_values(keys[1], (C1, C0 * 27), (C0 * 27) ** -0.5, 0.625),
        "kernel_two": normal_values(keys[2], (C2, C1 * 27), (C1 * 27) ** -0.5, 0.21875, ((0, 8),)),
        "cotangent": normal_values(keys[3], (SAMPLES, C2, DEPTH // 4, (HEIGHT // 4) * (WIDTH // 4)), 4.0, 24.0, ((0, 4), (1, 8), (2, 16))),
    }


LEAK_SLOPE = 0.3
CONV_DIMS = ("NCDHW", "OIDHW", "NCDHW")


def activate(values):
    return LEAK_SLOPE * values + (1.0 - LEAK_SLOPE) * jax.nn.softplus(values)


def slope_at(values):
    return LEAK_SLOPE + (1.0 - LEAK_SLOPE) * jax.nn.sigmoid(values)


def pooled(values):
    count, chans, dsize, hsize, wsize = values.shape
    blocks = values.reshape(count, chans, dsize // 2, 2, hsize // 2, 2, wsize // 2, 2)
    return blocks.mean(axis=(3, 5, 7))


def spread_up(values):
    values = jnp.repeat(jnp.repeat(jnp.repeat(values, 2, axis=2), 2, axis=3), 2, axis=4)
    return values * 0.125


def conv_same(inputs, kernel):
    return lax.conv_general_dilated(inputs, kernel, (1, 1, 1), ((1, 1), (1, 1), (1, 1)),
                                    dimension_numbers=CONV_DIMS, preferred_element_type=jnp.float32)


def one_sample(vol_one, first_kernel, second_kernel, cot_one):
    pre_one = conv_same(vol_one, first_kernel)
    level_one = pooled(activate(pre_one)).astype(jnp.bfloat16)
    pre_two = conv_same(level_one, second_kernel)
    pooled_out = pooled(activate(pre_two)).astype(jnp.bfloat16)
    delta_two = (spread_up(cot_one.astype(jnp.float32)) * slope_at(pre_two)).astype(jnp.bfloat16)
    padded = jnp.pad(level_one, ((0, 0), (0, 0), (1, 1), (1, 1), (1, 1)))
    weight_part = lax.conv_general_dilated(padded, delta_two, (1, 1, 1), "VALID",
                                           dimension_numbers=("CNDHW", "IODHW", "NCDHW"),
                                           preferred_element_type=jnp.float32)
    flipped = jnp.flip(second_kernel, axis=(2, 3, 4))
    back_grad = lax.conv_general_dilated(delta_two, flipped, (1, 1, 1), ((1, 1), (1, 1), (1, 1)),
                                         dimension_numbers=("NCDHW", "IODHW", "NCDHW"),
                                         preferred_element_type=jnp.float32)
    return pooled_out[0], weight_part, back_grad[0].astype(jnp.bfloat16)


def reference(volume, kernel_one, kernel_two, cotangent):
    first_kernel = kernel_one.reshape(C1, C0, 3, 3, 3)
    second_kernel = kernel_two.reshape(C2, C1, 3, 3, 3)

    def per_sample(items):
        vol_one, cot_one = items
        cot_grid = cot_one.reshape(1, C2, DEPTH // 4, HEIGHT // 4, WIDTH // 4)
        return one_sample(vol_one[None], first_kernel, second_kernel, cot_grid)

    pooled_all, weight_parts, act_all = lax.map(per_sample, (volume, cotangent))
    scale = 1.0 / (float(SAMPLES * (DEPTH // 2) * (HEIGHT // 2) * (WIDTH // 2)) ** 0.5)
    weight_sum = jnp.sum(weight_parts * scale, axis=0)
    weight_grad = jnp.transpose(weight_sum, (1, 0, 2, 3, 4)).reshape(C2, C1 * 27)
    pooled_two = pooled_all.reshape(SAMPLES, C2, DEPTH // 4, (HEIGHT // 4) * (WIDTH // 4))
    return pooled_two, weight_grad, act_all
```

```python
import jax
import jax.numpy as jnp
from jax import lax
from jax.sharding import PartitionSpec as P

LEAK_SLOPE = 0.3
CONV_DIMS = ("NCDHW", "OIDHW", "NCDHW")


def extended(block, sides, width):
    for axis, dim in sides:
        count = lax.axis_size(axis)
        forward = [(i, i + 1) for i in range(count - 1)]
        backward = [(target, source) for source, target in forward]
        low = lax.ppermute(
            lax.slice_in_dim(block, block.shape[dim] - width, None, axis=dim), axis, forward
        )
        high = lax.ppermute(lax.slice_in_dim(block, 0, width, axis=dim), axis, backward)
        block = jnp.concatenate([low, block, high], axis=dim)
    return block


def butterfly_sum(values, axes):
    sizes = [lax.axis_size(axis) for axis in axes]
    count = 1
    for size in sizes:
        count *= size
    if count & (count - 1):
        return lax.psum(values, axes)
    step = 1
    while step < count:
        pairs = [(i, i ^ step) for i in range(count)]
        values = values + lax.ppermute(values, axes, pairs)
        step *= 2
    return values


def halving_scatter(values, axis, dim):
    count = lax.axis_size(axis)
    if count & (count - 1):
        return lax.psum_scatter(values, axis, scatter_dimension=dim, tiled=True)
    index = lax.axis_index(axis)
    step = count // 2
    while step >= 1:
        half = values.shape[dim] // 2
        bit = (index // step) % 2
        keep = lax.dynamic_slice_in_dim(values, bit * half, half, axis=dim)
        send = lax.dynamic_slice_in_dim(values, (1 - bit) * half, half, axis=dim)
        pairs = [(i, i ^ step) for i in range(count)]
        values = keep + lax.ppermute(send, axis, pairs)
        step //= 2
    return values


def activate(values):
    return LEAK_SLOPE * values + (1.0 - LEAK_SLOPE) * jax.nn.softplus(values)


def slope_at(values):
    return LEAK_SLOPE + (1.0 - LEAK_SLOPE) * jax.nn.sigmoid(values)


def pooled(values):
    count, chans, dsize, hsize, wsize = values.shape
    blocks = values.reshape(count, chans, dsize // 2, 2, hsize // 2, 2, wsize // 2, 2)
    return blocks.mean(axis=(3, 5, 7))


def spread_up(values):
    values = jnp.repeat(jnp.repeat(jnp.repeat(values, 2, axis=2), 2, axis=3), 2, axis=4)
    return values * 0.125


def conv_valid(inputs, kernel):
    return lax.conv_general_dilated(
        inputs,
        kernel,
        (1, 1, 1),
        "VALID",
        dimension_numbers=CONV_DIMS,
        preferred_element_type=jnp.float32,
    )


def back_conv(delta_pad, kernel):
    flipped = jnp.flip(kernel, axis=(2, 3, 4))
    return lax.conv_general_dilated(
        delta_pad,
        flipped,
        (1, 1, 1),
        "VALID",
        dimension_numbers=("NCDHW", "IODHW", "NCDHW"),
        preferred_element_type=jnp.float32,
    )


def shards(volume, kernel_one, kernel_two, cotangent):
    depth_count = lax.axis_size("depth")
    height_count = lax.axis_size("height")
    sample_count = lax.axis_size("sample")
    chans_in = volume.shape[1]
    depth_loc = volume.shape[2]
    height_loc = volume.shape[3]
    width_all = volume.shape[4]
    chans_mid = kernel_one.shape[0]
    filters = kernel_two.shape[0]
    first_kernel = kernel_one.reshape(chans_mid, chans_in, 3, 3, 3)
    second_kernel = kernel_two.reshape(filters, chans_mid, 3, 3, 3)
    padded = extended(volume, (("depth", 2), ("height", 3)), 1)
    window = jnp.pad(padded, ((0, 0), (0, 0), (0, 0), (0, 0), (1, 1)))
    level_loc = pooled(activate(conv_valid(window, first_kernel))).astype(jnp.bfloat16)
    slab_rows = lax.all_gather(level_loc, "height", axis=3, tiled=True)
    level_one = extended(slab_rows, (("depth", 2),), 1)
    level_pad = jnp.pad(level_one, ((0, 0), (0, 0), (0, 0), (1, 1), (1, 1)))
    pre_two = conv_valid(level_pad, second_kernel)
    pooled_grid = pooled(activate(pre_two)).astype(jnp.bfloat16)
    depth_two = pooled_grid.shape[2]
    pooled_two = pooled_grid.reshape(
        1, filters, depth_two, pooled_grid.shape[3] * pooled_grid.shape[4]
    )
    cot_grid = cotangent.reshape(1, filters, depth_two, pooled_grid.shape[3], pooled_grid.shape[4])
    delta_two = (spread_up(cot_grid.astype(jnp.float32)) * slope_at(pre_two)).astype(jnp.bfloat16)
    weight_part = lax.conv_general_dilated(
        level_pad,
        delta_two,
        (1, 1, 1),
        "VALID",
        dimension_numbers=("CNDHW", "IODHW", "NCDHW"),
        preferred_element_type=jnp.float32,
    )
    total_cells = (
        sample_count
        * (depth_loc // 2)
        * depth_count
        * (height_loc // 2)
        * height_count
        * (width_all // 2)
    )
    scale = 1.0 / float(total_cells) ** 0.5
    weight_term = jnp.transpose(weight_part * scale, (1, 0, 2, 3, 4)).reshape(
        filters, chans_mid * 27
    )
    weight_grad = butterfly_sum(weight_term, ("depth", "sample"))
    delta_ext = extended(delta_two, (("depth", 2),), 1)
    delta_pad = jnp.pad(delta_ext, ((0, 0), (0, 0), (0, 0), (1, 1), (1, 1)))
    back_part = back_conv(delta_pad, second_kernel)
    act_grad = halving_scatter(back_part, "height", 3).astype(jnp.bfloat16)
    return (pooled_two, weight_grad, act_grad)


def solution(mesh):
    in_specs = (
        P("sample", None, "depth", "height", None),
        P(),
        P("height", None),
        P("sample", "height", "depth", None),
    )
    out_specs = (
        P("sample", "height", "depth", None),
        P("height", None),
        P("sample", None, "depth", "height", None),
    )
    return jax.shard_map(shards, mesh=mesh, in_specs=in_specs, out_specs=out_specs, check_vma=False)
```

```python
import jax
import jax.numpy as jnp
from jax import lax
from jax.sharding import PartitionSpec as P

LEAK_SLOPE = 0.3
CONV_DIMS = ("NCDHW", "OIDHW", "NCDHW")


def extended(block, sides, width):
    for axis, dim in sides:
        count = lax.axis_size(axis)
        forward = [(i, i + 1) for i in range(count - 1)]
        backward = [(target, source) for source, target in forward]
        low = lax.ppermute(
            lax.slice_in_dim(block, block.shape[dim] - width, None, axis=dim), axis, forward
        )
        high = lax.ppermute(lax.slice_in_dim(block, 0, width, axis=dim), axis, backward)
        block = jnp.concatenate([low, block, high], axis=dim)
    return block


def butterfly_sum(values, axes):
    sizes = [lax.axis_size(axis) for axis in axes]
    count = 1
    for size in sizes:
        count *= size
    if count & (count - 1):
        return lax.psum(values, axes)
    step = 1
    while step < count:
        pairs = [(i, i ^ step) for i in range(count)]
        values = values + lax.ppermute(values, axes, pairs)
        step *= 2
    return values


def halving_scatter(values, axis, dim):
    count = lax.axis_size(axis)
    if count & (count - 1):
        return lax.psum_scatter(values, axis, scatter_dimension=dim, tiled=True)
    index = lax.axis_index(axis)
    step = count // 2
    while step >= 1:
        half = values.shape[dim] // 2
        bit = (index // step) % 2
        keep = lax.dynamic_slice_in_dim(values, bit * half, half, axis=dim)
        send = lax.dynamic_slice_in_dim(values, (1 - bit) * half, half, axis=dim)
        pairs = [(i, i ^ step) for i in range(count)]
        values = keep + lax.ppermute(send, axis, pairs)
        step //= 2
    return values


def activate(values):
    return LEAK_SLOPE * values + (1.0 - LEAK_SLOPE) * jax.nn.softplus(values)


def slope_at(values):
    return LEAK_SLOPE + (1.0 - LEAK_SLOPE) * jax.nn.sigmoid(values)


def pooled(values):
    count, chans, dsize, hsize, wsize = values.shape
    blocks = values.reshape(count, chans, dsize // 2, 2, hsize // 2, 2, wsize // 2, 2)
    return blocks.mean(axis=(3, 5, 7))


def spread_up(values):
    values = jnp.repeat(jnp.repeat(jnp.repeat(values, 2, axis=2), 2, axis=3), 2, axis=4)
    return values * 0.125


def conv_valid(inputs, kernel):
    return lax.conv_general_dilated(
        inputs,
        kernel,
        (1, 1, 1),
        "VALID",
        dimension_numbers=CONV_DIMS,
        preferred_element_type=jnp.float32,
    )


def back_conv(delta_pad, kernel):
    flipped = jnp.flip(kernel, axis=(2, 3, 4))
    return lax.conv_general_dilated(
        delta_pad,
        flipped,
        (1, 1, 1),
        "VALID",
        dimension_numbers=("NCDHW", "IODHW", "NCDHW"),
        preferred_element_type=jnp.float32,
    )


def shards(volume, kernel_one, kernel_two, cotangent):
    depth_count = lax.axis_size("depth")
    height_count = lax.axis_size("height")
    sample_count = lax.axis_size("sample")
    chans_in = volume.shape[1]
    depth_loc = volume.shape[2]
    height_loc = volume.shape[3]
    width_all = volume.shape[4]
    chans_mid = kernel_one.shape[0]
    filters = kernel_two.shape[0]
    first_kernel = kernel_one.reshape(chans_mid, chans_in, 3, 3, 3)
    second_kernel = kernel_two.reshape(filters, chans_mid, 3, 3, 3)
    padded = extended(volume, (("depth", 2), ("height", 3)), 1)
    window = jnp.pad(padded, ((0, 0), (0, 0), (0, 0), (0, 0), (1, 1)))
    level_loc = pooled(activate(conv_valid(window, first_kernel))).astype(jnp.bfloat16)
    slab_rows = lax.all_gather(level_loc, "height", axis=3, tiled=True)
    level_one = extended(slab_rows, (("depth", 2),), 1)
    level_pad = jnp.pad(level_one, ((0, 0), (0, 0), (0, 0), (1, 1), (1, 1)))
    pre_two = conv_valid(level_pad, second_kernel)
    pooled_grid = pooled(activate(pre_two)).astype(jnp.bfloat16)
    depth_two = pooled_grid.shape[2]
    pooled_two = pooled_grid.reshape(
        1, filters, depth_two, pooled_grid.shape[3] * pooled_grid.shape[4]
    )
    cot_grid = cotangent.reshape(1, filters, depth_two, pooled_grid.shape[3], pooled_grid.shape[4])
    delta_two = (spread_up(cot_grid.astype(jnp.float32)) * slope_at(pre_two)).astype(jnp.bfloat16)
    weight_part = lax.conv_general_dilated(
        level_pad,
        delta_two,
        (1, 1, 1),
        "VALID",
        dimension_numbers=("CNDHW", "IODHW", "NCDHW"),
        preferred_element_type=jnp.float32,
    )
    total_cells = (
        sample_count
        * (depth_loc // 2)
        * depth_count
        * (height_loc // 2)
        * height_count
        * (width_all // 2)
    )
    scale = 1.0 / float(total_cells) ** 0.5
    weight_term = jnp.transpose(weight_part * scale, (1, 0, 2, 3, 4)).reshape(
        filters, chans_mid * 27
    )
    flat_size = weight_term.size
    lanes = 128 if flat_size % 128 == 0 else flat_size
    weight_grad = butterfly_sum(
        weight_term.reshape(flat_size // lanes, lanes), ("depth", "sample")
    ).reshape(weight_term.shape)
    delta_ext = extended(delta_two, (("depth", 2),), 1)
    delta_pad = jnp.pad(delta_ext, ((0, 0), (0, 0), (0, 0), (1, 1), (1, 1)))
    back_part = back_conv(delta_pad, second_kernel)
    act_grad = halving_scatter(back_part, "height", 3).astype(jnp.bfloat16)
    return (pooled_two, weight_grad, act_grad)


def solution(mesh):
    in_specs = (
        P("sample", None, "depth", "height", None),
        P(),
        P("height", None),
        P("sample", "height", "depth", None),
    )
    out_specs = (
        P("sample", "height", "depth", None),
        P("height", None),
        P("sample", None, "depth", "height", None),
    )
    return jax.shard_map(shards, mesh=mesh, in_specs=in_specs, out_specs=out_specs, check_vma=False)
```

```python
import jax
import jax.numpy as jnp
from jax import lax
from jax.sharding import PartitionSpec as P

LEAK_SLOPE = 0.3
CONV_DIMS = ("NCDHW", "OIDHW", "NCDHW")


def extended(block, sides, width):
    for axis, dim in sides:
        count = lax.axis_size(axis)
        forward = [(i, i + 1) for i in range(count - 1)]
        backward = [(target, source) for source, target in forward]
        low = lax.ppermute(
            lax.slice_in_dim(block, block.shape[dim] - width, None, axis=dim), axis, forward
        )
        high = lax.ppermute(lax.slice_in_dim(block, 0, width, axis=dim), axis, backward)
        block = jnp.concatenate([low, block, high], axis=dim)
    return block


def butterfly_sum(values, axes):
    sizes = [lax.axis_size(axis) for axis in axes]
    count = 1
    for size in sizes:
        count *= size
    if count & (count - 1):
        return lax.psum(values, axes)
    step = 1
    while step < count:
        pairs = [(i, i ^ step) for i in range(count)]
        values = values + lax.ppermute(values, axes, pairs)
        step *= 2
    return values


def halving_scatter(values, axis, dim):
    count = lax.axis_size(axis)
    if count & (count - 1):
        return lax.psum_scatter(values, axis, scatter_dimension=dim, tiled=True)
    index = lax.axis_index(axis)
    step = count // 2
    while step >= 1:
        half = values.shape[dim] // 2
        bit = (index // step) % 2
        keep = lax.dynamic_slice_in_dim(values, bit * half, half, axis=dim)
        send = lax.dynamic_slice_in_dim(values, (1 - bit) * half, half, axis=dim)
        pairs = [(i, i ^ step) for i in range(count)]
        values = keep + lax.ppermute(send, axis, pairs)
        step //= 2
    return values


def weight_gradient(level_ext, delta):
    _, chans, _, hsize, wsize = level_ext.shape
    _, filters, dsize, _, _ = delta.shape
    dpad = jnp.pad(delta[0], ((0, 0), (0, 0), (1, 1), (1, 1)))
    shifted = jnp.stack(
        [
            dpad[:, :, 2 - kh : 2 - kh + hsize, 2 - kw : 2 - kw + wsize]
            for kh in range(3)
            for kw in range(3)
        ],
        axis=1,
    )
    levels = jnp.stack([level_ext[0, :, kd : kd + dsize] for kd in range(3)], axis=0)
    grad = lax.dot_general(
        shifted,
        levels,
        (((2, 3, 4), (2, 3, 4)), ((), ())),
        preferred_element_type=jnp.float32,
    )
    grad = grad.reshape(filters, 3, 3, 3, chans)
    return jnp.transpose(grad, (0, 4, 3, 1, 2)).reshape(filters, chans * 27)


def activate(values):
    return LEAK_SLOPE * values + (1.0 - LEAK_SLOPE) * jax.nn.softplus(values)


def slope_at(values):
    return LEAK_SLOPE + (1.0 - LEAK_SLOPE) * jax.nn.sigmoid(values)


def pooled(values):
    count, chans, dsize, hsize, wsize = values.shape
    blocks = values.reshape(count, chans, dsize // 2, 2, hsize // 2, 2, wsize // 2, 2)
    return blocks.mean(axis=(3, 5, 7))


def spread_up(values):
    values = jnp.repeat(jnp.repeat(jnp.repeat(values, 2, axis=2), 2, axis=3), 2, axis=4)
    return values * 0.125


def conv_valid(inputs, kernel):
    return lax.conv_general_dilated(
        inputs,
        kernel,
        (1, 1, 1),
        "VALID",
        dimension_numbers=CONV_DIMS,
        preferred_element_type=jnp.float32,
    )


def back_conv(delta_pad, kernel):
    flipped = jnp.flip(kernel, axis=(2, 3, 4))
    return lax.conv_general_dilated(
        delta_pad,
        flipped,
        (1, 1, 1),
        "VALID",
        dimension_numbers=("NCDHW", "IODHW", "NCDHW"),
        preferred_element_type=jnp.float32,
    )


def shards(volume, kernel_one, kernel_two, cotangent):
    depth_count = lax.axis_size("depth")
    height_count = lax.axis_size("height")
    sample_count = lax.axis_size("sample")
    chans_in = volume.shape[1]
    depth_loc = volume.shape[2]
    height_loc = volume.shape[3]
    width_all = volume.shape[4]
    chans_mid = kernel_one.shape[0]
    filters = kernel_two.shape[0]
    first_kernel = kernel_one.reshape(chans_mid, chans_in, 3, 3, 3)
    second_kernel = kernel_two.reshape(filters, chans_mid, 3, 3, 3)
    padded = extended(volume, (("depth", 2), ("height", 3)), 1)
    window = jnp.pad(padded, ((0, 0), (0, 0), (0, 0), (0, 0), (1, 1)))
    level_loc = pooled(activate(conv_valid(window, first_kernel))).astype(jnp.bfloat16)
    slab_rows = lax.all_gather(level_loc, "height", axis=3, tiled=True)
    level_one = extended(slab_rows, (("depth", 2),), 1)
    level_pad = jnp.pad(level_one, ((0, 0), (0, 0), (0, 0), (1, 1), (1, 1)))
    pre_two = conv_valid(level_pad, second_kernel)
    pooled_grid = pooled(activate(pre_two)).astype(jnp.bfloat16)
    depth_two = pooled_grid.shape[2]
    pooled_two = pooled_grid.reshape(
        1, filters, depth_two, pooled_grid.shape[3] * pooled_grid.shape[4]
    )
    cot_grid = cotangent.reshape(1, filters, depth_two, pooled_grid.shape[3], pooled_grid.shape[4])
    delta_two = (spread_up(cot_grid.astype(jnp.float32)) * slope_at(pre_two)).astype(jnp.bfloat16)
    scale = 1.0 / float(
        sample_count
        * (depth_loc // 2)
        * depth_count
        * (height_loc // 2)
        * height_count
        * (width_all // 2)
    ) ** 0.5
    weight_term = weight_gradient(level_one, delta_two) * scale
    flat_size = weight_term.size
    lanes = 128 if flat_size % 128 == 0 else flat_size
    weight_grad = butterfly_sum(
        weight_term.reshape(flat_size // lanes, lanes), ("depth", "sample")
    ).reshape(weight_term.shape)
    delta_ext = extended(delta_two, (("depth", 2),), 1)
    delta_pad = jnp.pad(delta_ext, ((0, 0), (0, 0), (0, 0), (1, 1), (1, 1)))
    back_part = back_conv(delta_pad, second_kernel)
    act_grad = halving_scatter(back_part, "height", 3).astype(jnp.bfloat16)
    return (pooled_two, weight_grad, act_grad)


def solution(mesh):
    in_specs = (
        P("sample", None, "depth", "height", None),
        P(),
        P("height", None),
        P("sample", "height", "depth", None),
    )
    out_specs = (
        P("sample", "height", "depth", None),
        P("height", None),
        P("sample", None, "depth", "height", None),
    )
    return jax.shard_map(shards, mesh=mesh, in_specs=in_specs, out_specs=out_specs, check_vma=False)
```

```python
import jax
import jax.numpy as jnp
from jax import lax
from jax.sharding import PartitionSpec as P

LEAK_SLOPE = 0.3
CONV_DIMS = ("NCDHW", "OIDHW", "NCDHW")


def extended(block, sides, width):
    for axis, dim in sides:
        count = lax.axis_size(axis)
        forward = [(i, i + 1) for i in range(count - 1)]
        backward = [(target, source) for source, target in forward]
        low = lax.ppermute(
            lax.slice_in_dim(block, block.shape[dim] - width, None, axis=dim), axis, forward
        )
        high = lax.ppermute(lax.slice_in_dim(block, 0, width, axis=dim), axis, backward)
        block = jnp.concatenate([low, block, high], axis=dim)
    return block


def butterfly_sum(values, axes, group_bits=3):
    count = 1
    for axis in axes:
        count *= lax.axis_size(axis)
    if count & (count - 1):
        return lax.psum(values, axes)
    bits = count.bit_length() - 1
    low = 0
    while low < bits:
        width = min(group_bits, bits - low)
        level = {0: values}
        for offset in range(1, 1 << width):
            mask = offset << low
            pairs = [(i, i ^ mask) for i in range(count)]
            level[mask] = lax.ppermute(values, axes, pairs)
        for t in range(width):
            bit = 1 << (low + t)
            level = {m: v + level[m | bit] for m, v in level.items() if not m & bit}
        values = level[0]
        low += width
    return values


def halving_scatter(values, axis, dim):
    count = lax.axis_size(axis)
    if count & (count - 1):
        return lax.psum_scatter(values, axis, scatter_dimension=dim, tiled=True)
    index = lax.axis_index(axis)
    step = count // 2
    while step >= 1:
        half = values.shape[dim] // 2
        bit = (index // step) % 2
        keep = lax.dynamic_slice_in_dim(values, bit * half, half, axis=dim)
        send = lax.dynamic_slice_in_dim(values, (1 - bit) * half, half, axis=dim)
        pairs = [(i, i ^ step) for i in range(count)]
        values = keep + lax.ppermute(send, axis, pairs)
        step //= 2
    return values


def weight_gradient(level_ext, delta):
    _, chans, _, hsize, wsize = level_ext.shape
    _, filters, dsize, _, _ = delta.shape
    dpad = jnp.pad(delta[0], ((0, 0), (0, 0), (1, 1), (1, 1)))
    shifted = jnp.stack(
        [
            dpad[:, :, 2 - kh : 2 - kh + hsize, 2 - kw : 2 - kw + wsize]
            for kh in range(3)
            for kw in range(3)
        ],
        axis=1,
    )
    levels = jnp.stack([level_ext[0, :, kd : kd + dsize] for kd in range(3)], axis=0)
    grad = lax.dot_general(
        shifted,
        levels,
        (((2, 3, 4), (2, 3, 4)), ((), ())),
        preferred_element_type=jnp.float32,
    )
    grad = grad.reshape(filters, 3, 3, 3, chans)
    return jnp.transpose(grad, (0, 4, 3, 1, 2)).reshape(filters, chans * 27)


def activate(values):
    return LEAK_SLOPE * values + (1.0 - LEAK_SLOPE) * jax.nn.softplus(values)


def slope_at(values):
    return LEAK_SLOPE + (1.0 - LEAK_SLOPE) * jax.nn.sigmoid(values)


def pooled(values):
    count, chans, dsize, hsize, wsize = values.shape
    blocks = values.reshape(count, chans, dsize // 2, 2, hsize // 2, 2, wsize // 2, 2)
    return blocks.mean(axis=(3, 5, 7))


def spread_up(values):
    values = jnp.repeat(jnp.repeat(jnp.repeat(values, 2, axis=2), 2, axis=3), 2, axis=4)
    return values * 0.125


def conv_valid(inputs, kernel):
    return lax.conv_general_dilated(
        inputs,
        kernel,
        (1, 1, 1),
        "VALID",
        dimension_numbers=CONV_DIMS,
        preferred_element_type=jnp.float32,
    )


def back_conv(delta_pad, kernel):
    flipped = jnp.flip(kernel, axis=(2, 3, 4))
    return lax.conv_general_dilated(
        delta_pad,
        flipped,
        (1, 1, 1),
        "VALID",
        dimension_numbers=("NCDHW", "IODHW", "NCDHW"),
        preferred_element_type=jnp.float32,
    )


def shards(volume, kernel_one, kernel_two, cotangent):
    depth_count = lax.axis_size("depth")
    height_count = lax.axis_size("height")
    sample_count = lax.axis_size("sample")
    chans_in = volume.shape[1]
    depth_loc = volume.shape[2]
    height_loc = volume.shape[3]
    width_all = volume.shape[4]
    chans_mid = kernel_one.shape[0]
    filters = kernel_two.shape[0]
    first_kernel = kernel_one.reshape(chans_mid, chans_in, 3, 3, 3)
    second_kernel = kernel_two.reshape(filters, chans_mid, 3, 3, 3)
    padded = extended(volume, (("depth", 2), ("height", 3)), 1)
    window = jnp.pad(padded, ((0, 0), (0, 0), (0, 0), (0, 0), (1, 1)))
    level_loc = pooled(activate(conv_valid(window, first_kernel))).astype(jnp.bfloat16)
    slab_rows = lax.all_gather(level_loc, "height", axis=3, tiled=True)
    level_one = extended(slab_rows, (("depth", 2),), 1)
    level_pad = jnp.pad(level_one, ((0, 0), (0, 0), (0, 0), (1, 1), (1, 1)))
    pre_two = conv_valid(level_pad, second_kernel)
    pooled_grid = pooled(activate(pre_two)).astype(jnp.bfloat16)
    depth_two = pooled_grid.shape[2]
    pooled_two = pooled_grid.reshape(
        1, filters, depth_two, pooled_grid.shape[3] * pooled_grid.shape[4]
    )
    cot_grid = cotangent.reshape(1, filters, depth_two, pooled_grid.shape[3], pooled_grid.shape[4])
    delta_two = (spread_up(cot_grid.astype(jnp.float32)) * slope_at(pre_two)).astype(jnp.bfloat16)
    scale = 1.0 / float(
        sample_count
        * (depth_loc // 2)
        * depth_count
        * (height_loc // 2)
        * height_count
        * (width_all // 2)
    ) ** 0.5
    weight_term = weight_gradient(level_one, delta_two) * scale
    flat_size = weight_term.size
    lanes = 128 if flat_size % 128 == 0 else flat_size
    weight_grad = butterfly_sum(
        weight_term.reshape(flat_size // lanes, lanes), ("depth", "sample")
    ).reshape(weight_term.shape)
    delta_ext = extended(delta_two, (("depth", 2),), 1)
    delta_pad = jnp.pad(delta_ext, ((0, 0), (0, 0), (0, 0), (1, 1), (1, 1)))
    back_part = back_conv(delta_pad, second_kernel)
    act_grad = halving_scatter(back_part, "height", 3).astype(jnp.bfloat16)
    return (pooled_two, weight_grad, act_grad)


def solution(mesh):
    in_specs = (
        P("sample", None, "depth", "height", None),
        P(),
        P("height", None),
        P("sample", "height", "depth", None),
    )
    out_specs = (
        P("sample", "height", "depth", None),
        P("height", None),
        P("sample", None, "depth", "height", None),
    )
    return jax.shard_map(shards, mesh=mesh, in_specs=in_specs, out_specs=out_specs, check_vma=False)
```

```python
import jax
import jax.numpy as jnp
from jax import lax
from jax.sharding import PartitionSpec as P

LEAK_SLOPE = 0.3
CONV_DIMS = ("NCDHW", "OIDHW", "NCDHW")


def extended(block, sides, width):
    for axis, dim in sides:
        count = lax.axis_size(axis)
        forward = [(i, i + 1) for i in range(count - 1)]
        backward = [(target, source) for source, target in forward]
        low = lax.ppermute(
            lax.slice_in_dim(block, block.shape[dim] - width, None, axis=dim), axis, forward
        )
        high = lax.ppermute(lax.slice_in_dim(block, 0, width, axis=dim), axis, backward)
        block = jnp.concatenate([low, block, high], axis=dim)
    return block


def butterfly_sum(values, axes):
    sizes = [lax.axis_size(axis) for axis in axes]
    count = 1
    for size in sizes:
        count *= size
    if count & (count - 1):
        return lax.psum(values, axes)
    step = 1
    while step < count:
        pairs = [(i, i ^ step) for i in range(count)]
        values = values + lax.ppermute(values, axes, pairs)
        step *= 2
    return values


def halving_scatter(values, axis, dim):
    count = lax.axis_size(axis)
    if count & (count - 1):
        return lax.psum_scatter(values, axis, scatter_dimension=dim, tiled=True)
    index = lax.axis_index(axis)
    step = count // 2
    while step >= 1:
        half = values.shape[dim] // 2
        bit = (index // step) % 2
        keep = lax.dynamic_slice_in_dim(values, bit * half, half, axis=dim)
        send = lax.dynamic_slice_in_dim(values, (1 - bit) * half, half, axis=dim)
        pairs = [(i, i ^ step) for i in range(count)]
        values = keep + lax.ppermute(send, axis, pairs)
        step //= 2
    return values


def delta_shifts(delta_ext):
    _, _, _, hsize, wsize = delta_ext.shape
    dpad = jnp.pad(delta_ext[0], ((0, 0), (0, 0), (1, 1), (1, 1)))
    return jnp.stack(
        [
            dpad[:, :, 2 - kh : 2 - kh + hsize, 2 - kw : 2 - kw + wsize]
            for kh in range(3)
            for kw in range(3)
        ],
        axis=1,
    )


def weight_gradient(level_ext, shifted):
    chans = level_ext.shape[1]
    filters, _, dsize, _, _ = shifted.shape
    levels = jnp.stack([level_ext[0, :, kd : kd + dsize] for kd in range(3)], axis=0)
    grad = lax.dot_general(
        shifted,
        levels,
        (((2, 3, 4), (2, 3, 4)), ((), ())),
        preferred_element_type=jnp.float32,
    )
    grad = grad.reshape(filters, 3, 3, 3, chans)
    return jnp.transpose(grad, (0, 4, 3, 1, 2)).reshape(filters, chans * 27)


def back_product(shifts_ext, kernel):
    filters, chans = kernel.shape[:2]
    dsize = shifts_ext.shape[2] - 2
    stacked = jnp.stack(
        [shifts_ext[:, :, 2 - kd : 2 - kd + dsize] for kd in range(3)], axis=0
    )
    weights = jnp.transpose(kernel, (1, 2, 0, 3, 4)).reshape(chans, 3, filters, 9)
    grad = lax.dot_general(
        weights,
        stacked,
        (((1, 2, 3), (0, 1, 2)), ((), ())),
        preferred_element_type=jnp.float32,
    )
    return grad[None]


def activate(values):
    return LEAK_SLOPE * values + (1.0 - LEAK_SLOPE) * jax.nn.softplus(values)


def slope_at(values):
    return LEAK_SLOPE + (1.0 - LEAK_SLOPE) * jax.nn.sigmoid(values)


def pooled(values):
    count, chans, dsize, hsize, wsize = values.shape
    blocks = values.reshape(count, chans, dsize // 2, 2, hsize // 2, 2, wsize // 2, 2)
    return blocks.mean(axis=(3, 5, 7))


def spread_up(values):
    values = jnp.repeat(jnp.repeat(jnp.repeat(values, 2, axis=2), 2, axis=3), 2, axis=4)
    return values * 0.125


def conv_valid(inputs, kernel):
    return lax.conv_general_dilated(
        inputs,
        kernel,
        (1, 1, 1),
        "VALID",
        dimension_numbers=CONV_DIMS,
        preferred_element_type=jnp.float32,
    )


def back_conv(delta_pad, kernel):
    flipped = jnp.flip(kernel, axis=(2, 3, 4))
    return lax.conv_general_dilated(
        delta_pad,
        flipped,
        (1, 1, 1),
        "VALID",
        dimension_numbers=("NCDHW", "IODHW", "NCDHW"),
        preferred_element_type=jnp.float32,
    )


def shards(volume, kernel_one, kernel_two, cotangent):
    depth_count = lax.axis_size("depth")
    height_count = lax.axis_size("height")
    sample_count = lax.axis_size("sample")
    chans_in = volume.shape[1]
    depth_loc = volume.shape[2]
    height_loc = volume.shape[3]
    width_all = volume.shape[4]
    chans_mid = kernel_one.shape[0]
    filters = kernel_two.shape[0]
    first_kernel = kernel_one.reshape(chans_mid, chans_in, 3, 3, 3)
    second_kernel = kernel_two.reshape(filters, chans_mid, 3, 3, 3)
    padded = extended(volume, (("depth", 2), ("height", 3)), 1)
    window = jnp.pad(padded, ((0, 0), (0, 0), (0, 0), (0, 0), (1, 1)))
    level_loc = pooled(activate(conv_valid(window, first_kernel))).astype(jnp.bfloat16)
    slab_rows = lax.all_gather(level_loc, "height", axis=3, tiled=True)
    level_one = extended(slab_rows, (("depth", 2),), 1)
    level_pad = jnp.pad(level_one, ((0, 0), (0, 0), (0, 0), (1, 1), (1, 1)))
    pre_two = conv_valid(level_pad, second_kernel)
    pooled_grid = pooled(activate(pre_two)).astype(jnp.bfloat16)
    depth_two = pooled_grid.shape[2]
    pooled_two = pooled_grid.reshape(
        1, filters, depth_two, pooled_grid.shape[3] * pooled_grid.shape[4]
    )
    cot_grid = cotangent.reshape(1, filters, depth_two, pooled_grid.shape[3], pooled_grid.shape[4])
    delta_two = (spread_up(cot_grid.astype(jnp.float32)) * slope_at(pre_two)).astype(jnp.bfloat16)
    scale = 1.0 / float(
        sample_count
        * (depth_loc // 2)
        * depth_count
        * (height_loc // 2)
        * height_count
        * (width_all // 2)
    ) ** 0.5
    delta_ext = extended(delta_two, (("depth", 2),), 1)
    shifts_ext = delta_shifts(delta_ext)
    weight_term = weight_gradient(level_one, shifts_ext[:, :, 1:-1]) * scale
    flat_size = weight_term.size
    lanes = 128 if flat_size % 128 == 0 else flat_size
    weight_grad = butterfly_sum(
        weight_term.reshape(flat_size // lanes, lanes), ("depth", "sample")
    ).reshape(weight_term.shape)
    back_part = back_product(shifts_ext, second_kernel)
    act_grad = halving_scatter(back_part, "height", 3).astype(jnp.bfloat16)
    return (pooled_two, weight_grad, act_grad)


def solution(mesh):
    in_specs = (
        P("sample", None, "depth", "height", None),
        P(),
        P("height", None),
        P("sample", "height", "depth", None),
    )
    out_specs = (
        P("sample", "height", "depth", None),
        P("height", None),
        P("sample", None, "depth", "height", None),
    )
    return jax.shard_map(shards, mesh=mesh, in_specs=in_specs, out_specs=out_specs, check_vma=False)
```

```python
import jax
import jax.numpy as jnp
from jax import lax
from jax.sharding import PartitionSpec as P

LEAK_SLOPE = 0.3
CONV_DIMS = ("NCDHW", "OIDHW", "NCDHW")


def extended(block, sides, width):
    for axis, dim in sides:
        count = lax.axis_size(axis)
        forward = [(i, i + 1) for i in range(count - 1)]
        backward = [(target, source) for source, target in forward]
        low = lax.ppermute(
            lax.slice_in_dim(block, block.shape[dim] - width, None, axis=dim), axis, forward
        )
        high = lax.ppermute(lax.slice_in_dim(block, 0, width, axis=dim), axis, backward)
        block = jnp.concatenate([low, block, high], axis=dim)
    return block


def butterfly_sum(values, axes):
    sizes = [lax.axis_size(axis) for axis in axes]
    count = 1
    for size in sizes:
        count *= size
    if count & (count - 1):
        return lax.psum(values, axes)
    step = 1
    while step < count:
        pairs = [(i, i ^ step) for i in range(count)]
        values = values + lax.ppermute(values, axes, pairs)
        step *= 2
    return values


def halving_scatter(values, axis, dim):
    count = lax.axis_size(axis)
    if count & (count - 1):
        return lax.psum_scatter(values, axis, scatter_dimension=dim, tiled=True)
    index = lax.axis_index(axis)
    step = count // 2
    while step >= 1:
        half = values.shape[dim] // 2
        bit = (index // step) % 2
        keep = lax.dynamic_slice_in_dim(values, bit * half, half, axis=dim)
        send = lax.dynamic_slice_in_dim(values, (1 - bit) * half, half, axis=dim)
        pairs = [(i, i ^ step) for i in range(count)]
        values = keep + lax.ppermute(send, axis, pairs)
        step //= 2
    return values


def weight_gradient(level_ext, delta):
    _, chans, _, hsize, wsize = level_ext.shape
    _, filters, dsize, _, _ = delta.shape
    dpad = jnp.pad(delta[0], ((0, 0), (0, 0), (1, 1), (1, 1)))
    shifted = jnp.stack(
        [
            dpad[:, :, 2 - kh : 2 - kh + hsize, 2 - kw : 2 - kw + wsize]
            for kh in range(3)
            for kw in range(3)
        ],
        axis=1,
    )
    levels = jnp.stack([level_ext[0, :, kd : kd + dsize] for kd in range(3)], axis=0)
    grad = lax.dot_general(
        shifted,
        levels,
        (((2, 3, 4), (2, 3, 4)), ((), ())),
        preferred_element_type=jnp.float32,
    )
    grad = grad.reshape(filters, 3, 3, 3, chans)
    return jnp.transpose(grad, (0, 4, 3, 1, 2)).reshape(filters, chans * 27)


def doubling_gather(block, axis, dim):
    count = lax.axis_size(axis)
    if count & (count - 1):
        return lax.all_gather(block, axis, axis=dim, tiled=True)
    index = lax.axis_index(axis)
    step = 1
    while step < count:
        pairs = [(i, i ^ step) for i in range(count)]
        other = lax.ppermute(block, axis, pairs)
        upper = (index // step) % 2 == 1
        low = jnp.where(upper, other, block)
        high = jnp.where(upper, block, other)
        block = jnp.concatenate([low, high], axis=dim)
        step *= 2
    return block


def activate(values):
    return LEAK_SLOPE * values + (1.0 - LEAK_SLOPE) * jax.nn.softplus(values)


def slope_at(values):
    return LEAK_SLOPE + (1.0 - LEAK_SLOPE) * jax.nn.sigmoid(values)


def pooled(values):
    count, chans, dsize, hsize, wsize = values.shape
    blocks = values.reshape(count, chans, dsize // 2, 2, hsize // 2, 2, wsize // 2, 2)
    return blocks.mean(axis=(3, 5, 7))


def spread_up(values):
    values = jnp.repeat(jnp.repeat(jnp.repeat(values, 2, axis=2), 2, axis=3), 2, axis=4)
    return values * 0.125


def conv_valid(inputs, kernel):
    return lax.conv_general_dilated(
        inputs,
        kernel,
        (1, 1, 1),
        "VALID",
        dimension_numbers=CONV_DIMS,
        preferred_element_type=jnp.float32,
    )


def back_conv(delta_pad, kernel):
    flipped = jnp.flip(kernel, axis=(2, 3, 4))
    return lax.conv_general_dilated(
        delta_pad,
        flipped,
        (1, 1, 1),
        "VALID",
        dimension_numbers=("NCDHW", "IODHW", "NCDHW"),
        preferred_element_type=jnp.float32,
    )


def shards(volume, kernel_one, kernel_two, cotangent):
    depth_count = lax.axis_size("depth")
    height_count = lax.axis_size("height")
    sample_count = lax.axis_size("sample")
    chans_in = volume.shape[1]
    depth_loc = volume.shape[2]
    height_loc = volume.shape[3]
    width_all = volume.shape[4]
    chans_mid = kernel_one.shape[0]
    filters = kernel_two.shape[0]
    first_kernel = kernel_one.reshape(chans_mid, chans_in, 3, 3, 3)
    second_kernel = kernel_two.reshape(filters, chans_mid, 3, 3, 3)
    padded = extended(volume, (("depth", 2), ("height", 3)), 1)
    window = jnp.pad(padded, ((0, 0), (0, 0), (0, 0), (0, 0), (1, 1)))
    level_loc = pooled(activate(conv_valid(window, first_kernel))).astype(jnp.bfloat16)
    slab_rows = doubling_gather(level_loc, "height", 3)
    level_one = extended(slab_rows, (("depth", 2),), 1)
    level_pad = jnp.pad(level_one, ((0, 0), (0, 0), (0, 0), (1, 1), (1, 1)))
    pre_two = conv_valid(level_pad, second_kernel)
    pooled_grid = pooled(activate(pre_two)).astype(jnp.bfloat16)
    depth_two = pooled_grid.shape[2]
    pooled_two = pooled_grid.reshape(
        1, filters, depth_two, pooled_grid.shape[3] * pooled_grid.shape[4]
    )
    cot_grid = cotangent.reshape(1, filters, depth_two, pooled_grid.shape[3], pooled_grid.shape[4])
    delta_two = (spread_up(cot_grid.astype(jnp.float32)) * slope_at(pre_two)).astype(jnp.bfloat16)
    scale = 1.0 / float(
        sample_count
        * (depth_loc // 2)
        * depth_count
        * (height_loc // 2)
        * height_count
        * (width_all // 2)
    ) ** 0.5
    weight_term = weight_gradient(level_one, delta_two) * scale
    flat_size = weight_term.size
    lanes = 128 if flat_size % 128 == 0 else flat_size
    weight_grad = butterfly_sum(
        weight_term.reshape(flat_size // lanes, lanes), ("depth", "sample")
    ).reshape(weight_term.shape)
    delta_ext = extended(delta_two, (("depth", 2),), 1)
    delta_pad = jnp.pad(delta_ext, ((0, 0), (0, 0), (0, 0), (1, 1), (1, 1)))
    back_part = back_conv(delta_pad, second_kernel)
    act_grad = halving_scatter(back_part, "height", 3).astype(jnp.bfloat16)
    return (pooled_two, weight_grad, act_grad)


def solution(mesh):
    in_specs = (
        P("sample", None, "depth", "height", None),
        P(),
        P("height", None),
        P("sample", "height", "depth", None),
    )
    out_specs = (
        P("sample", "height", "depth", None),
        P("height", None),
        P("sample", None, "depth", "height", None),
    )
    return jax.shard_map(shards, mesh=mesh, in_specs=in_specs, out_specs=out_specs, check_vma=False)
```

```python
import jax
import jax.numpy as jnp
from jax import lax
from jax.sharding import PartitionSpec as P

LEAK_SLOPE = 0.3
CONV_DIMS = ("NCDHW", "OIDHW", "NCDHW")


def extended(block, sides, width):
    for axis, dim in sides:
        count = lax.axis_size(axis)
        forward = [(i, i + 1) for i in range(count - 1)]
        backward = [(target, source) for source, target in forward]
        low = lax.ppermute(
            lax.slice_in_dim(block, block.shape[dim] - width, None, axis=dim), axis, forward
        )
        high = lax.ppermute(lax.slice_in_dim(block, 0, width, axis=dim), axis, backward)
        block = jnp.concatenate([low, block, high], axis=dim)
    return block


def butterfly_sum(values, axes):
    sizes = [lax.axis_size(axis) for axis in axes]
    count = 1
    for size in sizes:
        count *= size
    if count & (count - 1):
        return lax.psum(values, axes)
    step = 1
    while step < count:
        pairs = [(i, i ^ step) for i in range(count)]
        values = values + lax.ppermute(values, axes, pairs)
        step *= 2
    return values


def halving_scatter(values, axis, dim):
    count = lax.axis_size(axis)
    if count & (count - 1):
        return lax.psum_scatter(values, axis, scatter_dimension=dim, tiled=True)
    index = lax.axis_index(axis)
    step = count // 2
    while step >= 1:
        half = values.shape[dim] // 2
        bit = (index // step) % 2
        keep = lax.dynamic_slice_in_dim(values, bit * half, half, axis=dim)
        send = lax.dynamic_slice_in_dim(values, (1 - bit) * half, half, axis=dim)
        pairs = [(i, i ^ step) for i in range(count)]
        values = keep + lax.ppermute(send, axis, pairs)
        step //= 2
    return values


def delta_shifts(delta_ext):
    _, _, _, hsize, wsize = delta_ext.shape
    dpad = jnp.pad(delta_ext[0], ((0, 0), (0, 0), (1, 1), (1, 1)))
    return jnp.stack(
        [
            dpad[:, :, 2 - kh : 2 - kh + hsize, 2 - kw : 2 - kw + wsize]
            for kh in range(3)
            for kw in range(3)
        ],
        axis=1,
    )


def weight_gradient(level_ext, shifted):
    chans = level_ext.shape[1]
    filters, _, dsize, _, _ = shifted.shape
    levels = jnp.stack([level_ext[0, :, kd : kd + dsize] for kd in range(3)], axis=0)
    grad = lax.dot_general(
        shifted,
        levels,
        (((2, 3, 4), (2, 3, 4)), ((), ())),
        preferred_element_type=jnp.float32,
    )
    grad = grad.reshape(filters, 3, 3, 3, chans)
    return jnp.transpose(grad, (0, 4, 3, 1, 2)).reshape(filters, chans * 27)


def back_product(shifts_ext, kernel):
    filters, chans = kernel.shape[:2]
    dsize = shifts_ext.shape[2] - 2
    stacked = jnp.stack(
        [shifts_ext[:, :, 2 - kd : 2 - kd + dsize] for kd in range(3)], axis=0
    )
    weights = jnp.transpose(kernel, (1, 2, 0, 3, 4)).reshape(chans, 3, filters, 9)
    grad = lax.dot_general(
        weights,
        stacked,
        (((1, 2, 3), (0, 1, 2)), ((), ())),
        preferred_element_type=jnp.float32,
    )
    return grad[None]


def activate(values):
    return LEAK_SLOPE * values + (1.0 - LEAK_SLOPE) * jax.nn.softplus(values)


def slope_at(values):
    return LEAK_SLOPE + (1.0 - LEAK_SLOPE) * jax.nn.sigmoid(values)


def pooled(values):
    count, chans, dsize, hsize, wsize = values.shape
    blocks = values.reshape(count, chans, dsize // 2, 2, hsize // 2, 2, wsize // 2, 2)
    return blocks.mean(axis=(3, 5, 7))


def spread_up(values):
    values = jnp.repeat(jnp.repeat(jnp.repeat(values, 2, axis=2), 2, axis=3), 2, axis=4)
    return values * 0.125


def conv_valid(inputs, kernel):
    return lax.conv_general_dilated(
        inputs,
        kernel,
        (1, 1, 1),
        "VALID",
        dimension_numbers=CONV_DIMS,
        preferred_element_type=jnp.float32,
    )


def back_conv(delta_pad, kernel):
    flipped = jnp.flip(kernel, axis=(2, 3, 4))
    return lax.conv_general_dilated(
        delta_pad,
        flipped,
        (1, 1, 1),
        "VALID",
        dimension_numbers=("NCDHW", "IODHW", "NCDHW"),
        preferred_element_type=jnp.float32,
    )


def shards(volume, kernel_one, kernel_two, cotangent):
    depth_count = lax.axis_size("depth")
    height_count = lax.axis_size("height")
    sample_count = lax.axis_size("sample")
    chans_in = volume.shape[1]
    depth_loc = volume.shape[2]
    height_loc = volume.shape[3]
    width_all = volume.shape[4]
    chans_mid = kernel_one.shape[0]
    filters = kernel_two.shape[0]
    first_kernel = kernel_one.reshape(chans_mid, chans_in, 3, 3, 3)
    second_kernel = kernel_two.reshape(filters, chans_mid, 3, 3, 3)
    padded = extended(volume, (("depth", 2), ("height", 3)), 1)
    window = jnp.pad(padded, ((0, 0), (0, 0), (0, 0), (0, 0), (1, 1)))
    level_loc = pooled(activate(conv_valid(window, first_kernel))).astype(jnp.bfloat16)
    slab_rows = lax.all_gather(level_loc, "height", axis=3, tiled=True)
    level_one = extended(slab_rows, (("depth", 2),), 1)
    level_pad = jnp.pad(level_one, ((0, 0), (0, 0), (0, 0), (1, 1), (1, 1)))
    pre_two = conv_valid(level_pad, second_kernel)
    pooled_grid = pooled(activate(pre_two)).astype(jnp.bfloat16)
    depth_two = pooled_grid.shape[2]
    pooled_two = pooled_grid.reshape(
        1, filters, depth_two, pooled_grid.shape[3] * pooled_grid.shape[4]
    )
    cot_grid = cotangent.reshape(1, filters, depth_two, pooled_grid.shape[3], pooled_grid.shape[4])
    delta_two = (spread_up(cot_grid.astype(jnp.float32)) * slope_at(pre_two)).astype(jnp.bfloat16)
    scale = 1.0 / float(
        sample_count
        * (depth_loc // 2)
        * depth_count
        * (height_loc // 2)
        * height_count
        * (width_all // 2)
    ) ** 0.5
    delta_ext = extended(delta_two, (("depth", 2),), 1)
    shifts_ext = delta_shifts(delta_ext)
    weight_term = weight_gradient(level_one, delta_shifts(delta_two)) * scale
    flat_size = weight_term.size
    lanes = 128 if flat_size % 128 == 0 else flat_size
    weight_grad = butterfly_sum(
        weight_term.reshape(flat_size // lanes, lanes), ("depth", "sample")
    ).reshape(weight_term.shape)
    back_part = back_product(shifts_ext, second_kernel)
    act_grad = halving_scatter(back_part, "height", 3).astype(jnp.bfloat16)
    return (pooled_two, weight_grad, act_grad)


def solution(mesh):
    in_specs = (
        P("sample", None, "depth", "height", None),
        P(),
        P("height", None),
        P("sample", "height", "depth", None),
    )
    out_specs = (
        P("sample", "height", "depth", None),
        P("height", None),
        P("sample", None, "depth", "height", None),
    )
    return jax.shard_map(shards, mesh=mesh, in_specs=in_specs, out_specs=out_specs, check_vma=False)
```

```python
import jax
import jax.numpy as jnp
from jax import lax
from jax.sharding import PartitionSpec as P

LEAK_SLOPE = 0.3
CONV_DIMS = ("NCDHW", "OIDHW", "NCDHW")


def extended(block, sides, width):
    for axis, dim in sides:
        count = lax.axis_size(axis)
        forward = [(i, i + 1) for i in range(count - 1)]
        backward = [(target, source) for source, target in forward]
        low = lax.ppermute(
            lax.slice_in_dim(block, block.shape[dim] - width, None, axis=dim), axis, forward
        )
        high = lax.ppermute(lax.slice_in_dim(block, 0, width, axis=dim), axis, backward)
        block = jnp.concatenate([low, block, high], axis=dim)
    return block


def butterfly_sum(values, axes):
    sizes = [lax.axis_size(axis) for axis in axes]
    count = 1
    for size in sizes:
        count *= size
    if count & (count - 1):
        return lax.psum(values, axes)
    step = 1
    while step < count:
        pairs = [(i, i ^ step) for i in range(count)]
        values = values + lax.ppermute(values, axes, pairs)
        step *= 2
    return values


def halving_scatter(values, axis, dim):
    count = lax.axis_size(axis)
    if count & (count - 1):
        return lax.psum_scatter(values, axis, scatter_dimension=dim, tiled=True)
    index = lax.axis_index(axis)
    step = count // 2
    while step >= 1:
        half = values.shape[dim] // 2
        bit = (index // step) % 2
        keep = lax.dynamic_slice_in_dim(values, bit * half, half, axis=dim)
        send = lax.dynamic_slice_in_dim(values, (1 - bit) * half, half, axis=dim)
        pairs = [(i, i ^ step) for i in range(count)]
        values = keep + lax.ppermute(send, axis, pairs)
        step //= 2
    return values


def delta_shifts(delta_ext):
    _, _, _, hsize, wsize = delta_ext.shape
    dpad = jnp.pad(delta_ext[0], ((0, 0), (0, 0), (1, 1), (1, 1)))
    return jnp.stack(
        [
            dpad[:, :, 2 - kh : 2 - kh + hsize, 2 - kw : 2 - kw + wsize]
            for kh in range(3)
            for kw in range(3)
        ],
        axis=1,
    )


def weight_gradient(level_ext, shifted):
    chans = level_ext.shape[1]
    filters, _, dsize, _, _ = shifted.shape
    levels = jnp.stack([level_ext[0, :, kd : kd + dsize] for kd in range(3)], axis=0)
    grad = lax.dot_general(
        shifted,
        levels,
        (((2, 3, 4), (2, 3, 4)), ((), ())),
        preferred_element_type=jnp.float32,
    )
    grad = grad.reshape(filters, 3, 3, 3, chans)
    return jnp.transpose(grad, (0, 4, 3, 1, 2)).reshape(filters, chans * 27)


def back_product(shifts_ext, kernel):
    filters, chans = kernel.shape[:2]
    dsize = shifts_ext.shape[2] - 2
    stacked = jnp.stack(
        [shifts_ext[:, :, 2 - kd : 2 - kd + dsize] for kd in range(3)], axis=0
    )
    weights = jnp.transpose(kernel, (1, 2, 0, 3, 4)).reshape(chans, 3, filters, 9)
    grad = lax.dot_general(
        weights,
        stacked,
        (((1, 2, 3), (0, 1, 2)), ((), ())),
        preferred_element_type=jnp.float32,
    )
    return grad[None]


def forward_product(level_ext, kernel):
    filters, chans = kernel.shape[:2]
    dsize = level_ext.shape[2] - 2
    shifts = delta_shifts(level_ext)
    stacked = jnp.stack([shifts[:, :, kd : kd + dsize] for kd in range(3)], axis=0)
    flipped = jnp.flip(kernel, axis=(3, 4))
    weights = jnp.transpose(flipped, (0, 2, 1, 3, 4)).reshape(filters, 3, chans, 9)
    grad = lax.dot_general(
        weights,
        stacked,
        (((1, 2, 3), (0, 1, 2)), ((), ())),
        preferred_element_type=jnp.float32,
    )
    return grad[None]


def activate(values):
    return LEAK_SLOPE * values + (1.0 - LEAK_SLOPE) * jax.nn.softplus(values)


def slope_at(values):
    return LEAK_SLOPE + (1.0 - LEAK_SLOPE) * jax.nn.sigmoid(values)


def pooled(values):
    count, chans, dsize, hsize, wsize = values.shape
    blocks = values.reshape(count, chans, dsize // 2, 2, hsize // 2, 2, wsize // 2, 2)
    return blocks.mean(axis=(3, 5, 7))


def spread_up(values):
    values = jnp.repeat(jnp.repeat(jnp.repeat(values, 2, axis=2), 2, axis=3), 2, axis=4)
    return values * 0.125


def conv_valid(inputs, kernel):
    return lax.conv_general_dilated(
        inputs,
        kernel,
        (1, 1, 1),
        "VALID",
        dimension_numbers=CONV_DIMS,
        preferred_element_type=jnp.float32,
    )


def back_conv(delta_pad, kernel):
    flipped = jnp.flip(kernel, axis=(2, 3, 4))
    return lax.conv_general_dilated(
        delta_pad,
        flipped,
        (1, 1, 1),
        "VALID",
        dimension_numbers=("NCDHW", "IODHW", "NCDHW"),
        preferred_element_type=jnp.float32,
    )


def shards(volume, kernel_one, kernel_two, cotangent):
    depth_count = lax.axis_size("depth")
    height_count = lax.axis_size("height")
    sample_count = lax.axis_size("sample")
    chans_in = volume.shape[1]
    depth_loc = volume.shape[2]
    height_loc = volume.shape[3]
    width_all = volume.shape[4]
    chans_mid = kernel_one.shape[0]
    filters = kernel_two.shape[0]
    first_kernel = kernel_one.reshape(chans_mid, chans_in, 3, 3, 3)
    second_kernel = kernel_two.reshape(filters, chans_mid, 3, 3, 3)
    padded = extended(volume, (("depth", 2), ("height", 3)), 1)
    window = jnp.pad(padded, ((0, 0), (0, 0), (0, 0), (0, 0), (1, 1)))
    level_loc = pooled(activate(conv_valid(window, first_kernel))).astype(jnp.bfloat16)
    slab_rows = lax.all_gather(level_loc, "height", axis=3, tiled=True)
    level_one = extended(slab_rows, (("depth", 2),), 1)
    pre_two = forward_product(level_one, second_kernel)
    pooled_grid = pooled(activate(pre_two)).astype(jnp.bfloat16)
    depth_two = pooled_grid.shape[2]
    pooled_two = pooled_grid.reshape(
        1, filters, depth_two, pooled_grid.shape[3] * pooled_grid.shape[4]
    )
    cot_grid = cotangent.reshape(1, filters, depth_two, pooled_grid.shape[3], pooled_grid.shape[4])
    delta_two = (spread_up(cot_grid.astype(jnp.float32)) * slope_at(pre_two)).astype(jnp.bfloat16)
    scale = 1.0 / float(
        sample_count
        * (depth_loc // 2)
        * depth_count
        * (height_loc // 2)
        * height_count
        * (width_all // 2)
    ) ** 0.5
    delta_ext = extended(delta_two, (("depth", 2),), 1)
    shifts_ext = delta_shifts(delta_ext)
    weight_term = weight_gradient(level_one, delta_shifts(delta_two)) * scale
    flat_size = weight_term.size
    lanes = 128 if flat_size % 128 == 0 else flat_size
    weight_grad = butterfly_sum(
        weight_term.reshape(flat_size // lanes, lanes), ("depth", "sample")
    ).reshape(weight_term.shape)
    back_part = back_product(shifts_ext, second_kernel)
    act_grad = halving_scatter(back_part, "height", 3).astype(jnp.bfloat16)
    return (pooled_two, weight_grad, act_grad)


def solution(mesh):
    in_specs = (
        P("sample", None, "depth", "height", None),
        P(),
        P("height", None),
        P("sample", "height", "depth", None),
    )
    out_specs = (
        P("sample", "height", "depth", None),
        P("height", None),
        P("sample", None, "depth", "height", None),
    )
    return jax.shard_map(shards, mesh=mesh, in_specs=in_specs, out_specs=out_specs, check_vma=False)
```

```python
import jax
import jax.numpy as jnp
from jax import lax
from jax.sharding import PartitionSpec as P

LEAK_SLOPE = 0.3
CONV_DIMS = ("NCDHW", "OIDHW", "NCDHW")


def extended(block, sides, width):
    for axis, dim in sides:
        count = lax.axis_size(axis)
        forward = [(i, i + 1) for i in range(count - 1)]
        backward = [(target, source) for source, target in forward]
        low = lax.ppermute(
            lax.slice_in_dim(block, block.shape[dim] - width, None, axis=dim), axis, forward
        )
        high = lax.ppermute(lax.slice_in_dim(block, 0, width, axis=dim), axis, backward)
        block = jnp.concatenate([low, block, high], axis=dim)
    return block


def butterfly_sum(values, axes):
    sizes = [lax.axis_size(axis) for axis in axes]
    count = 1
    for size in sizes:
        count *= size
    if count & (count - 1):
        return lax.psum(values, axes)
    step = 1
    while step < count:
        pairs = [(i, i ^ step) for i in range(count)]
        values = values + lax.ppermute(values, axes, pairs)
        step *= 2
    return values


def halving_scatter(values, axis, dim):
    count = lax.axis_size(axis)
    if count & (count - 1):
        return lax.psum_scatter(values, axis, scatter_dimension=dim, tiled=True)
    index = lax.axis_index(axis)
    step = count // 2
    while step >= 1:
        half = values.shape[dim] // 2
        bit = (index // step) % 2
        keep = lax.dynamic_slice_in_dim(values, bit * half, half, axis=dim)
        send = lax.dynamic_slice_in_dim(values, (1 - bit) * half, half, axis=dim)
        pairs = [(i, i ^ step) for i in range(count)]
        values = keep + lax.ppermute(send, axis, pairs)
        step //= 2
    return values


def delta_shifts(delta_ext):
    _, _, _, hsize, wsize = delta_ext.shape
    dpad = jnp.pad(delta_ext[0], ((0, 0), (0, 0), (1, 1), (1, 1)))
    return jnp.stack(
        [
            dpad[:, :, 2 - kh : 2 - kh + hsize, 2 - kw : 2 - kw + wsize]
            for kh in range(3)
            for kw in range(3)
        ],
        axis=1,
    )


def weight_gradient(level_ext, shifted):
    chans = level_ext.shape[1]
    filters, _, dsize, _, _ = shifted.shape
    levels = jnp.stack([level_ext[0, :, kd : kd + dsize] for kd in range(3)], axis=0)
    grad = lax.dot_general(
        shifted,
        levels,
        (((2, 3, 4), (2, 3, 4)), ((), ())),
        preferred_element_type=jnp.float32,
    )
    grad = grad.reshape(filters, 3, 3, 3, chans)
    return jnp.transpose(grad, (0, 4, 3, 1, 2)).reshape(filters, chans * 27)


def back_product(shifts_ext, kernel):
    filters, chans = kernel.shape[:2]
    dsize = shifts_ext.shape[2] - 2
    stacked = jnp.stack(
        [shifts_ext[:, :, 2 - kd : 2 - kd + dsize] for kd in range(3)], axis=0
    )
    weights = jnp.transpose(kernel, (1, 2, 0, 3, 4)).reshape(chans, 3, filters, 9)
    grad = lax.dot_general(
        weights,
        stacked,
        (((1, 2, 3), (0, 1, 2)), ((), ())),
        preferred_element_type=jnp.float32,
    )
    return grad[None]


def forward_product(level_ext, kernel):
    filters, chans = kernel.shape[:2]
    dsize = level_ext.shape[2] - 2
    shifts = delta_shifts(level_ext)
    stacked = jnp.stack([shifts[:, :, kd : kd + dsize] for kd in range(3)], axis=0)
    flipped = jnp.flip(kernel, axis=(3, 4))
    weights = jnp.transpose(flipped, (0, 2, 1, 3, 4)).reshape(filters, 3, chans, 9)
    grad = lax.dot_general(
        weights,
        stacked,
        (((1, 2, 3), (0, 1, 2)), ((), ())),
        preferred_element_type=jnp.float32,
    )
    return grad[None]


def near_first_scatter(values, axis):
    count = lax.axis_size(axis)
    chans, dsize, hsize, wsize = values.shape[1:]
    if count & (count - 1):
        return lax.psum_scatter(values, axis, scatter_dimension=3, tiled=True)
    bits = count.bit_length() - 1
    rows = hsize // count
    index = lax.axis_index(axis)
    grid = jnp.transpose(values[0], (2, 1, 0, 3))
    grid = grid.reshape((2,) * bits + (rows, dsize, chans, wsize))
    for t in range(bits):
        axis_pos = bits - 1 - t
        bit = (index >> t) & 1
        keep = lax.dynamic_slice_in_dim(grid, bit, 1, axis=axis_pos)
        send = lax.dynamic_slice_in_dim(grid, 1 - bit, 1, axis=axis_pos)
        pairs = [(i, i ^ (1 << t)) for i in range(count)]
        grid = jnp.squeeze(keep + lax.ppermute(send, axis, pairs), axis_pos)
    return jnp.transpose(grid, (2, 1, 0, 3))[None]


def activate(values):
    return LEAK_SLOPE * values + (1.0 - LEAK_SLOPE) * jax.nn.softplus(values)


def slope_at(values):
    return LEAK_SLOPE + (1.0 - LEAK_SLOPE) * jax.nn.sigmoid(values)


def pooled(values):
    count, chans, dsize, hsize, wsize = values.shape
    blocks = values.reshape(count, chans, dsize // 2, 2, hsize // 2, 2, wsize // 2, 2)
    return blocks.mean(axis=(3, 5, 7))


def spread_up(values):
    values = jnp.repeat(jnp.repeat(jnp.repeat(values, 2, axis=2), 2, axis=3), 2, axis=4)
    return values * 0.125


def conv_valid(inputs, kernel):
    return lax.conv_general_dilated(
        inputs,
        kernel,
        (1, 1, 1),
        "VALID",
        dimension_numbers=CONV_DIMS,
        preferred_element_type=jnp.float32,
    )


def back_conv(delta_pad, kernel):
    flipped = jnp.flip(kernel, axis=(2, 3, 4))
    return lax.conv_general_dilated(
        delta_pad,
        flipped,
        (1, 1, 1),
        "VALID",
        dimension_numbers=("NCDHW", "IODHW", "NCDHW"),
        preferred_element_type=jnp.float32,
    )


def shards(volume, kernel_one, kernel_two, cotangent):
    depth_count = lax.axis_size("depth")
    height_count = lax.axis_size("height")
    sample_count = lax.axis_size("sample")
    chans_in = volume.shape[1]
    depth_loc = volume.shape[2]
    height_loc = volume.shape[3]
    width_all = volume.shape[4]
    chans_mid = kernel_one.shape[0]
    filters = kernel_two.shape[0]
    first_kernel = kernel_one.reshape(chans_mid, chans_in, 3, 3, 3)
    second_kernel = kernel_two.reshape(filters, chans_mid, 3, 3, 3)
    padded = extended(volume, (("depth", 2), ("height", 3)), 1)
    window = jnp.pad(padded, ((0, 0), (0, 0), (0, 0), (0, 0), (1, 1)))
    level_loc = pooled(activate(conv_valid(window, first_kernel))).astype(jnp.bfloat16)
    slab_rows = lax.all_gather(level_loc, "height", axis=3, tiled=True)
    level_one = extended(slab_rows, (("depth", 2),), 1)
    pre_two = forward_product(level_one, second_kernel)
    pooled_grid = pooled(activate(pre_two)).astype(jnp.bfloat16)
    depth_two = pooled_grid.shape[2]
    pooled_two = pooled_grid.reshape(
        1, filters, depth_two, pooled_grid.shape[3] * pooled_grid.shape[4]
    )
    cot_grid = cotangent.reshape(1, filters, depth_two, pooled_grid.shape[3], pooled_grid.shape[4])
    delta_two = (spread_up(cot_grid.astype(jnp.float32)) * slope_at(pre_two)).astype(jnp.bfloat16)
    scale = 1.0 / float(
        sample_count
        * (depth_loc // 2)
        * depth_count
        * (height_loc // 2)
        * height_count
        * (width_all // 2)
    ) ** 0.5
    delta_ext = extended(delta_two, (("depth", 2),), 1)
    shifts_ext = delta_shifts(delta_ext)
    weight_term = weight_gradient(level_one, delta_shifts(delta_two)) * scale
    flat_size = weight_term.size
    lanes = 128 if flat_size % 128 == 0 else flat_size
    weight_grad = butterfly_sum(
        weight_term.reshape(flat_size // lanes, lanes), ("depth", "sample")
    ).reshape(weight_term.shape)
    back_part = back_product(shifts_ext, second_kernel)
    act_grad = near_first_scatter(back_part, "height").astype(jnp.bfloat16)
    return (pooled_two, weight_grad, act_grad)


def solution(mesh):
    in_specs = (
        P("sample", None, "depth", "height", None),
        P(),
        P("height", None),
        P("sample", "height", "depth", None),
    )
    out_specs = (
        P("sample", "height", "depth", None),
        P("height", None),
        P("sample", None, "depth", "height", None),
    )
    return jax.shard_map(shards, mesh=mesh, in_specs=in_specs, out_specs=out_specs, check_vma=False)
```

```python
import jax
import jax.numpy as jnp
from jax import lax
from jax.sharding import PartitionSpec as P

LEAK_SLOPE = 0.3
CONV_DIMS = ("NCDHW", "OIDHW", "NCDHW")


def extended(block, sides, width):
    for axis, dim in sides:
        count = lax.axis_size(axis)
        forward = [(i, i + 1) for i in range(count - 1)]
        backward = [(target, source) for source, target in forward]
        low = lax.ppermute(
            lax.slice_in_dim(block, block.shape[dim] - width, None, axis=dim), axis, forward
        )
        high = lax.ppermute(lax.slice_in_dim(block, 0, width, axis=dim), axis, backward)
        block = jnp.concatenate([low, block, high], axis=dim)
    return block


def butterfly_sum(values, axes):
    sizes = [lax.axis_size(axis) for axis in axes]
    count = 1
    for size in sizes:
        count *= size
    if count & (count - 1):
        return lax.psum(values, axes)
    step = 1
    while step < count:
        pairs = [(i, i ^ step) for i in range(count)]
        values = values + lax.ppermute(values, axes, pairs)
        step *= 2
    return values


def halving_scatter(values, axis, dim):
    count = lax.axis_size(axis)
    if count & (count - 1):
        return lax.psum_scatter(values, axis, scatter_dimension=dim, tiled=True)
    index = lax.axis_index(axis)
    step = count // 2
    while step >= 1:
        half = values.shape[dim] // 2
        bit = (index // step) % 2
        keep = lax.dynamic_slice_in_dim(values, bit * half, half, axis=dim)
        send = lax.dynamic_slice_in_dim(values, (1 - bit) * half, half, axis=dim)
        pairs = [(i, i ^ step) for i in range(count)]
        values = keep + lax.ppermute(send, axis, pairs)
        step //= 2
    return values


def delta_shifts(delta_ext):
    _, _, _, hsize, wsize = delta_ext.shape
    dpad = jnp.pad(delta_ext[0], ((0, 0), (0, 0), (1, 1), (1, 1)))
    return jnp.stack(
        [
            dpad[:, :, 2 - kh : 2 - kh + hsize, 2 - kw : 2 - kw + wsize]
            for kh in range(3)
            for kw in range(3)
        ],
        axis=1,
    )


def weight_gradient(level_ext, shifted):
    chans = level_ext.shape[1]
    filters, _, dsize, _, _ = shifted.shape
    levels = jnp.stack([level_ext[0, :, kd : kd + dsize] for kd in range(3)], axis=0)
    grad = lax.dot_general(
        shifted,
        levels,
        (((2, 3, 4), (2, 3, 4)), ((), ())),
        preferred_element_type=jnp.float32,
    )
    grad = grad.reshape(filters, 3, 3, 3, chans)
    return jnp.transpose(grad, (0, 4, 3, 1, 2)).reshape(filters, chans * 27)


def back_product(shifts_ext, kernel):
    filters, chans = kernel.shape[:2]
    dsize = shifts_ext.shape[2] - 2
    stacked = jnp.stack(
        [shifts_ext[:, :, 2 - kd : 2 - kd + dsize] for kd in range(3)], axis=0
    )
    weights = jnp.transpose(kernel, (1, 2, 0, 3, 4)).reshape(chans, 3, filters, 9)
    grad = lax.dot_general(
        weights,
        stacked,
        (((1, 2, 3), (0, 1, 2)), ((), ())),
        preferred_element_type=jnp.float32,
    )
    return grad[None]


def forward_product(level_ext, kernel):
    filters, chans = kernel.shape[:2]
    dsize = level_ext.shape[2] - 2
    shifts = delta_shifts(level_ext)
    stacked = jnp.stack([shifts[:, :, kd : kd + dsize] for kd in range(3)], axis=0)
    flipped = jnp.flip(kernel, axis=(3, 4))
    weights = jnp.transpose(flipped, (0, 2, 1, 3, 4)).reshape(filters, 3, chans, 9)
    grad = lax.dot_general(
        weights,
        stacked,
        (((1, 2, 3), (0, 1, 2)), ((), ())),
        preferred_element_type=jnp.float32,
    )
    return grad[None]


def near_first_scatter(values, axis):
    count = lax.axis_size(axis)
    chans, dsize, hsize, wsize = values.shape[1:]
    if count & (count - 1):
        return lax.psum_scatter(values, axis, scatter_dimension=3, tiled=True)
    bits = count.bit_length() - 1
    rows = hsize // count
    index = lax.axis_index(axis)
    grid = jnp.transpose(values[0], (2, 1, 0, 3))
    grid = grid.reshape((2,) * bits + (rows, dsize, chans, wsize))
    for t in range(bits):
        axis_pos = bits - 1 - t
        bit = (index >> t) & 1
        keep = lax.dynamic_slice_in_dim(grid, bit, 1, axis=axis_pos)
        send = lax.dynamic_slice_in_dim(grid, 1 - bit, 1, axis=axis_pos)
        pairs = [(i, i ^ (1 << t)) for i in range(count)]
        grid = jnp.squeeze(keep + lax.ppermute(send, axis, pairs), axis_pos)
    return jnp.transpose(grid, (2, 1, 0, 3))[None]


def activate(values):
    return LEAK_SLOPE * values + (1.0 - LEAK_SLOPE) * jax.nn.softplus(values)


def slope_at(values):
    return LEAK_SLOPE + (1.0 - LEAK_SLOPE) * jax.nn.sigmoid(values)


def pooled(values):
    count, chans, dsize, hsize, wsize = values.shape
    blocks = values.reshape(count, chans, dsize // 2, 2, hsize // 2, 2, wsize // 2, 2)
    return blocks.mean(axis=(3, 5, 7))


def spread_up(values):
    values = jnp.repeat(jnp.repeat(jnp.repeat(values, 2, axis=2), 2, axis=3), 2, axis=4)
    return values * 0.125


def conv_valid(inputs, kernel):
    return lax.conv_general_dilated(
        inputs,
        kernel,
        (1, 1, 1),
        "VALID",
        dimension_numbers=CONV_DIMS,
        preferred_element_type=jnp.float32,
    )


def back_conv(delta_pad, kernel):
    flipped = jnp.flip(kernel, axis=(2, 3, 4))
    return lax.conv_general_dilated(
        delta_pad,
        flipped,
        (1, 1, 1),
        "VALID",
        dimension_numbers=("NCDHW", "IODHW", "NCDHW"),
        preferred_element_type=jnp.float32,
    )


def shards(volume, kernel_one, kernel_two, cotangent):
    depth_count = lax.axis_size("depth")
    height_count = lax.axis_size("height")
    sample_count = lax.axis_size("sample")
    chans_in = volume.shape[1]
    depth_loc = volume.shape[2]
    height_loc = volume.shape[3]
    width_all = volume.shape[4]
    chans_mid = kernel_one.shape[0]
    filters = kernel_two.shape[0]
    first_kernel = kernel_one.reshape(chans_mid, chans_in, 3, 3, 3)
    second_kernel = kernel_two.reshape(filters, chans_mid, 3, 3, 3)
    padded = extended(volume, (("depth", 2), ("height", 3)), 1)
    pre_one = forward_product(padded, first_kernel)[:, :, :, 1:-1]
    level_loc = pooled(activate(pre_one)).astype(jnp.bfloat16)
    slab_rows = lax.all_gather(level_loc, "height", axis=3, tiled=True)
    level_one = extended(slab_rows, (("depth", 2),), 1)
    pre_two = forward_product(level_one, second_kernel)
    pooled_grid = pooled(activate(pre_two)).astype(jnp.bfloat16)
    depth_two = pooled_grid.shape[2]
    pooled_two = pooled_grid.reshape(
        1, filters, depth_two, pooled_grid.shape[3] * pooled_grid.shape[4]
    )
    cot_grid = cotangent.reshape(1, filters, depth_two, pooled_grid.shape[3], pooled_grid.shape[4])
    delta_two = (spread_up(cot_grid.astype(jnp.float32)) * slope_at(pre_two)).astype(jnp.bfloat16)
    scale = 1.0 / float(
        sample_count
        * (depth_loc // 2)
        * depth_count
        * (height_loc // 2)
        * height_count
        * (width_all // 2)
    ) ** 0.5
    delta_ext = extended(delta_two, (("depth", 2),), 1)
    shifts_ext = delta_shifts(delta_ext)
    weight_term = weight_gradient(level_one, delta_shifts(delta_two)) * scale
    flat_size = weight_term.size
    lanes = 128 if flat_size % 128 == 0 else flat_size
    weight_grad = butterfly_sum(
        weight_term.reshape(flat_size // lanes, lanes), ("depth", "sample")
    ).reshape(weight_term.shape)
    back_part = back_product(shifts_ext, second_kernel)
    act_grad = near_first_scatter(back_part, "height").astype(jnp.bfloat16)
    return (pooled_two, weight_grad, act_grad)


def solution(mesh):
    in_specs = (
        P("sample", None, "depth", "height", None),
        P(),
        P("height", None),
        P("sample", "height", "depth", None),
    )
    out_specs = (
        P("sample", "height", "depth", None),
        P("height", None),
        P("sample", None, "depth", "height", None),
    )
    return jax.shard_map(shards, mesh=mesh, in_specs=in_specs, out_specs=out_specs, check_vma=False)
```

```python
import jax
import jax.numpy as jnp
from jax import lax
from jax.sharding import PartitionSpec as P

LEAK_SLOPE = 0.3
CONV_DIMS = ("NCDHW", "OIDHW", "NCDHW")


def extended(block, sides, width):
    for axis, dim in sides:
        count = lax.axis_size(axis)
        forward = [(i, i + 1) for i in range(count - 1)]
        backward = [(target, source) for source, target in forward]
        low = lax.ppermute(
            lax.slice_in_dim(block, block.shape[dim] - width, None, axis=dim), axis, forward
        )
        high = lax.ppermute(lax.slice_in_dim(block, 0, width, axis=dim), axis, backward)
        block = jnp.concatenate([low, block, high], axis=dim)
    return block


def butterfly_sum(values, axes):
    sizes = [lax.axis_size(axis) for axis in axes]
    count = 1
    for size in sizes:
        count *= size
    if count & (count - 1):
        return lax.psum(values, axes)
    step = 1
    while step < count:
        pairs = [(i, i ^ step) for i in range(count)]
        values = values + lax.ppermute(values, axes, pairs)
        step *= 2
    return values


def halving_scatter(values, axis, dim):
    count = lax.axis_size(axis)
    if count & (count - 1):
        return lax.psum_scatter(values, axis, scatter_dimension=dim, tiled=True)
    index = lax.axis_index(axis)
    step = count // 2
    while step >= 1:
        half = values.shape[dim] // 2
        bit = (index // step) % 2
        keep = lax.dynamic_slice_in_dim(values, bit * half, half, axis=dim)
        send = lax.dynamic_slice_in_dim(values, (1 - bit) * half, half, axis=dim)
        pairs = [(i, i ^ step) for i in range(count)]
        values = keep + lax.ppermute(send, axis, pairs)
        step //= 2
    return values


def delta_shifts(delta_ext):
    _, _, _, hsize, wsize = delta_ext.shape
    dpad = jnp.pad(delta_ext[0], ((0, 0), (0, 0), (1, 1), (1, 1)))
    return jnp.stack(
        [
            dpad[:, :, 2 - kh : 2 - kh + hsize, 2 - kw : 2 - kw + wsize]
            for kh in range(3)
            for kw in range(3)
        ],
        axis=1,
    )


def weight_gradient(level_ext, shifted):
    chans = level_ext.shape[1]
    filters, _, dsize, _, _ = shifted.shape
    levels = jnp.stack([level_ext[0, :, kd : kd + dsize] for kd in range(3)], axis=0)
    grad = lax.dot_general(
        shifted,
        levels,
        (((2, 3, 4), (2, 3, 4)), ((), ())),
        preferred_element_type=jnp.float32,
    )
    grad = grad.reshape(filters, 3, 3, 3, chans)
    return jnp.transpose(grad, (0, 4, 3, 1, 2)).reshape(filters, chans * 27)


def back_product(shifts_ext, kernel):
    filters, chans = kernel.shape[:2]
    dsize = shifts_ext.shape[2] - 2
    stacked = jnp.stack(
        [shifts_ext[:, :, 2 - kd : 2 - kd + dsize] for kd in range(3)], axis=0
    )
    weights = jnp.transpose(kernel, (1, 2, 0, 3, 4)).reshape(chans, 3, filters, 9)
    grad = lax.dot_general(
        weights,
        stacked,
        (((1, 2, 3), (0, 1, 2)), ((), ())),
        preferred_element_type=jnp.float32,
    )
    return grad[None]


def forward_product(level_ext, kernel):
    filters, chans = kernel.shape[:2]
    dsize = level_ext.shape[2] - 2
    shifts = delta_shifts(level_ext)
    stacked = jnp.stack([shifts[:, :, kd : kd + dsize] for kd in range(3)], axis=0)
    flipped = jnp.flip(kernel, axis=(3, 4))
    weights = jnp.transpose(flipped, (0, 2, 1, 3, 4)).reshape(filters, 3, chans, 9)
    grad = lax.dot_general(
        weights,
        stacked,
        (((1, 2, 3), (0, 1, 2)), ((), ())),
        preferred_element_type=jnp.float32,
    )
    return grad[None]


def near_first_scatter(values, axis):
    count = lax.axis_size(axis)
    chans, dsize, hsize, wsize = values.shape[1:]
    if count & (count - 1):
        return lax.psum_scatter(values, axis, scatter_dimension=3, tiled=True)
    bits = count.bit_length() - 1
    rows = hsize // count
    index = lax.axis_index(axis)
    grid = jnp.transpose(values[0], (2, 1, 0, 3))
    grid = grid.reshape((2,) * bits + (rows, dsize, chans, wsize))
    for t in range(bits):
        axis_pos = bits - 1 - t
        bit = (index >> t) & 1
        keep = lax.dynamic_slice_in_dim(grid, bit, 1, axis=axis_pos)
        send = lax.dynamic_slice_in_dim(grid, 1 - bit, 1, axis=axis_pos)
        pairs = [(i, i ^ (1 << t)) for i in range(count)]
        grid = jnp.squeeze(keep + lax.ppermute(send, axis, pairs), axis_pos)
    return jnp.transpose(grid, (2, 1, 0, 3))[None]


def first_product(volume_ext, kernel):
    filters, chans = kernel.shape[:2]
    _, _, dext, hext, wsize = volume_ext.shape
    dsize, hsize = dext - 2, hext - 2
    merged = volume_ext.reshape(1, chans, 1, dext * hext, wsize)
    shifts = delta_shifts(merged)[:, :, 0]
    stacked = jnp.stack(
        [shifts[:, :, kd * hext : (kd + dsize) * hext] for kd in range(3)], axis=0
    )
    flipped = jnp.flip(kernel, axis=(3, 4))
    weights = jnp.transpose(flipped, (0, 2, 1, 3, 4)).reshape(filters, 3, chans, 9)
    grad = lax.dot_general(
        weights,
        stacked,
        (((1, 2, 3), (0, 1, 2)), ((), ())),
        preferred_element_type=jnp.float32,
    )
    grad = grad.reshape(1, filters, dsize, hext, wsize)
    return grad[:, :, :, 1 : 1 + hsize]


def activate(values):
    return LEAK_SLOPE * values + (1.0 - LEAK_SLOPE) * jax.nn.softplus(values)


def slope_at(values):
    return LEAK_SLOPE + (1.0 - LEAK_SLOPE) * jax.nn.sigmoid(values)


def pooled(values):
    count, chans, dsize, hsize, wsize = values.shape
    blocks = values.reshape(count, chans, dsize // 2, 2, hsize // 2, 2, wsize // 2, 2)
    return blocks.mean(axis=(3, 5, 7))


def spread_up(values):
    values = jnp.repeat(jnp.repeat(jnp.repeat(values, 2, axis=2), 2, axis=3), 2, axis=4)
    return values * 0.125


def conv_valid(inputs, kernel):
    return lax.conv_general_dilated(
        inputs,
        kernel,
        (1, 1, 1),
        "VALID",
        dimension_numbers=CONV_DIMS,
        preferred_element_type=jnp.float32,
    )


def back_conv(delta_pad, kernel):
    flipped = jnp.flip(kernel, axis=(2, 3, 4))
    return lax.conv_general_dilated(
        delta_pad,
        flipped,
        (1, 1, 1),
        "VALID",
        dimension_numbers=("NCDHW", "IODHW", "NCDHW"),
        preferred_element_type=jnp.float32,
    )


def shards(volume, kernel_one, kernel_two, cotangent):
    depth_count = lax.axis_size("depth")
    height_count = lax.axis_size("height")
    sample_count = lax.axis_size("sample")
    chans_in = volume.shape[1]
    depth_loc = volume.shape[2]
    height_loc = volume.shape[3]
    width_all = volume.shape[4]
    chans_mid = kernel_one.shape[0]
    filters = kernel_two.shape[0]
    first_kernel = kernel_one.reshape(chans_mid, chans_in, 3, 3, 3)
    second_kernel = kernel_two.reshape(filters, chans_mid, 3, 3, 3)
    padded = extended(volume, (("depth", 2), ("height", 3)), 1)
    pre_one = first_product(padded, first_kernel)
    level_loc = pooled(activate(pre_one)).astype(jnp.bfloat16)
    slab_rows = lax.all_gather(level_loc, "height", axis=3, tiled=True)
    level_one = extended(slab_rows, (("depth", 2),), 1)
    pre_two = forward_product(level_one, second_kernel)
    pooled_grid = pooled(activate(pre_two)).astype(jnp.bfloat16)
    depth_two = pooled_grid.shape[2]
    pooled_two = pooled_grid.reshape(
        1, filters, depth_two, pooled_grid.shape[3] * pooled_grid.shape[4]
    )
    cot_grid = cotangent.reshape(1, filters, depth_two, pooled_grid.shape[3], pooled_grid.shape[4])
    delta_two = (spread_up(cot_grid.astype(jnp.float32)) * slope_at(pre_two)).astype(jnp.bfloat16)
    scale = 1.0 / float(
        sample_count
        * (depth_loc // 2)
        * depth_count
        * (height_loc // 2)
        * height_count
        * (width_all // 2)
    ) ** 0.5
    delta_ext = extended(delta_two, (("depth", 2),), 1)
    shifts_ext = delta_shifts(delta_ext)
    weight_term = weight_gradient(level_one, delta_shifts(delta_two)) * scale
    flat_size = weight_term.size
    lanes = 128 if flat_size % 128 == 0 else flat_size
    weight_grad = butterfly_sum(
        weight_term.reshape(flat_size // lanes, lanes), ("depth", "sample")
    ).reshape(weight_term.shape)
    back_part = back_product(shifts_ext, second_kernel)
    act_grad = near_first_scatter(back_part, "height").astype(jnp.bfloat16)
    return (pooled_two, weight_grad, act_grad)


def solution(mesh):
    in_specs = (
        P("sample", None, "depth", "height", None),
        P(),
        P("height", None),
        P("sample", "height", "depth", None),
    )
    out_specs = (
        P("sample", "height", "depth", None),
        P("height", None),
        P("sample", None, "depth", "height", None),
    )
    return jax.shard_map(shards, mesh=mesh, in_specs=in_specs, out_specs=out_specs, check_vma=False)
```

```python
import jax
import jax.numpy as jnp
from jax import lax
from jax.sharding import PartitionSpec as P

LEAK_SLOPE = 0.3
CONV_DIMS = ("NCDHW", "OIDHW", "NCDHW")


def extended(block, sides, width):
    for axis, dim in sides:
        count = lax.axis_size(axis)
        forward = [(i, i + 1) for i in range(count - 1)]
        backward = [(target, source) for source, target in forward]
        low = lax.ppermute(
            lax.slice_in_dim(block, block.shape[dim] - width, None, axis=dim), axis, forward
        )
        high = lax.ppermute(lax.slice_in_dim(block, 0, width, axis=dim), axis, backward)
        block = jnp.concatenate([low, block, high], axis=dim)
    return block


def butterfly_sum(values, axes):
    sizes = [lax.axis_size(axis) for axis in axes]
    count = 1
    for size in sizes:
        count *= size
    if count & (count - 1):
        return lax.psum(values, axes)
    inner = lax.axis_size(axes[-1])

    def label(i):
        low = i % inner
        return i - low + (low ^ (low >> 1))

    owner = {label(i): i for i in range(count)}
    step = 1
    while step < count:
        pairs = [(i, owner[label(i) ^ step]) for i in range(count)]
        values = values + lax.ppermute(values, axes, pairs)
        step *= 2
    return values


def halving_scatter(values, axis, dim):
    count = lax.axis_size(axis)
    if count & (count - 1):
        return lax.psum_scatter(values, axis, scatter_dimension=dim, tiled=True)
    index = lax.axis_index(axis)
    step = count // 2
    while step >= 1:
        half = values.shape[dim] // 2
        bit = (index // step) % 2
        keep = lax.dynamic_slice_in_dim(values, bit * half, half, axis=dim)
        send = lax.dynamic_slice_in_dim(values, (1 - bit) * half, half, axis=dim)
        pairs = [(i, i ^ step) for i in range(count)]
        values = keep + lax.ppermute(send, axis, pairs)
        step //= 2
    return values


def delta_shifts(delta_ext):
    _, _, _, hsize, wsize = delta_ext.shape
    dpad = jnp.pad(delta_ext[0], ((0, 0), (0, 0), (1, 1), (1, 1)))
    return jnp.stack(
        [
            dpad[:, :, 2 - kh : 2 - kh + hsize, 2 - kw : 2 - kw + wsize]
            for kh in range(3)
            for kw in range(3)
        ],
        axis=1,
    )


def weight_gradient(level_ext, shifted):
    chans = level_ext.shape[1]
    filters, _, dsize, _, _ = shifted.shape
    levels = jnp.stack([level_ext[0, :, kd : kd + dsize] for kd in range(3)], axis=0)
    grad = lax.dot_general(
        shifted,
        levels,
        (((2, 3, 4), (2, 3, 4)), ((), ())),
        preferred_element_type=jnp.float32,
    )
    grad = grad.reshape(filters, 3, 3, 3, chans)
    return jnp.transpose(grad, (0, 4, 3, 1, 2)).reshape(filters, chans * 27)


def back_product(shifts_ext, kernel):
    filters, chans = kernel.shape[:2]
    dsize = shifts_ext.shape[2] - 2
    stacked = jnp.stack(
        [shifts_ext[:, :, 2 - kd : 2 - kd + dsize] for kd in range(3)], axis=0
    )
    weights = jnp.transpose(kernel, (1, 2, 0, 3, 4)).reshape(chans, 3, filters, 9)
    grad = lax.dot_general(
        weights,
        stacked,
        (((1, 2, 3), (0, 1, 2)), ((), ())),
        preferred_element_type=jnp.float32,
    )
    return grad[None]


def forward_product(level_ext, kernel):
    filters, chans = kernel.shape[:2]
    dsize = level_ext.shape[2] - 2
    shifts = delta_shifts(level_ext)
    stacked = jnp.stack([shifts[:, :, kd : kd + dsize] for kd in range(3)], axis=0)
    flipped = jnp.flip(kernel, axis=(3, 4))
    weights = jnp.transpose(flipped, (0, 2, 1, 3, 4)).reshape(filters, 3, chans, 9)
    grad = lax.dot_general(
        weights,
        stacked,
        (((1, 2, 3), (0, 1, 2)), ((), ())),
        preferred_element_type=jnp.float32,
    )
    return grad[None]


def near_first_scatter(values, axis):
    count = lax.axis_size(axis)
    chans, dsize, hsize, wsize = values.shape[1:]
    if count & (count - 1):
        return lax.psum_scatter(values, axis, scatter_dimension=3, tiled=True)
    bits = count.bit_length() - 1
    rows = hsize // count
    index = lax.axis_index(axis)
    grid = jnp.transpose(values[0], (2, 1, 0, 3))
    grid = grid.reshape((2,) * bits + (rows, dsize, chans, wsize))
    for t in range(bits):
        axis_pos = bits - 1 - t
        bit = (index >> t) & 1
        keep = lax.dynamic_slice_in_dim(grid, bit, 1, axis=axis_pos)
        send = lax.dynamic_slice_in_dim(grid, 1 - bit, 1, axis=axis_pos)
        pairs = [(i, i ^ (1 << t)) for i in range(count)]
        grid = jnp.squeeze(keep + lax.ppermute(send, axis, pairs), axis_pos)
    return jnp.transpose(grid, (2, 1, 0, 3))[None]


def activate(values):
    return LEAK_SLOPE * values + (1.0 - LEAK_SLOPE) * jax.nn.softplus(values)


def slope_at(values):
    return LEAK_SLOPE + (1.0 - LEAK_SLOPE) * jax.nn.sigmoid(values)


def pooled(values):
    count, chans, dsize, hsize, wsize = values.shape
    blocks = values.reshape(count, chans, dsize // 2, 2, hsize // 2, 2, wsize // 2, 2)
    return blocks.mean(axis=(3, 5, 7))


def spread_up(values):
    values = jnp.repeat(jnp.repeat(jnp.repeat(values, 2, axis=2), 2, axis=3), 2, axis=4)
    return values * 0.125


def conv_valid(inputs, kernel):
    return lax.conv_general_dilated(
        inputs,
        kernel,
        (1, 1, 1),
        "VALID",
        dimension_numbers=CONV_DIMS,
        preferred_element_type=jnp.float32,
    )


def back_conv(delta_pad, kernel):
    flipped = jnp.flip(kernel, axis=(2, 3, 4))
    return lax.conv_general_dilated(
        delta_pad,
        flipped,
        (1, 1, 1),
        "VALID",
        dimension_numbers=("NCDHW", "IODHW", "NCDHW"),
        preferred_element_type=jnp.float32,
    )


def shards(volume, kernel_one, kernel_two, cotangent):
    depth_count = lax.axis_size("depth")
    height_count = lax.axis_size("height")
    sample_count = lax.axis_size("sample")
    chans_in = volume.shape[1]
    depth_loc = volume.shape[2]
    height_loc = volume.shape[3]
    width_all = volume.shape[4]
    chans_mid = kernel_one.shape[0]
    filters = kernel_two.shape[0]
    first_kernel = kernel_one.reshape(chans_mid, chans_in, 3, 3, 3)
    second_kernel = kernel_two.reshape(filters, chans_mid, 3, 3, 3)
    padded = extended(volume, (("depth", 2), ("height", 3)), 1)
    pre_one = forward_product(padded, first_kernel)[:, :, :, 1:-1]
    level_loc = pooled(activate(pre_one)).astype(jnp.bfloat16)
    slab_rows = lax.all_gather(level_loc, "height", axis=3, tiled=True)
    level_one = extended(slab_rows, (("depth", 2),), 1)
    pre_two = forward_product(level_one, second_kernel)
    pooled_grid = pooled(activate(pre_two)).astype(jnp.bfloat16)
    depth_two = pooled_grid.shape[2]
    pooled_two = pooled_grid.reshape(
        1, filters, depth_two, pooled_grid.shape[3] * pooled_grid.shape[4]
    )
    cot_grid = cotangent.reshape(1, filters, depth_two, pooled_grid.shape[3], pooled_grid.shape[4])
    delta_two = (spread_up(cot_grid.astype(jnp.float32)) * slope_at(pre_two)).astype(jnp.bfloat16)
    scale = 1.0 / float(
        sample_count
        * (depth_loc // 2)
        * depth_count
        * (height_loc // 2)
        * height_count
        * (width_all // 2)
    ) ** 0.5
    delta_ext = extended(delta_two, (("depth", 2),), 1)
    shifts_ext = delta_shifts(delta_ext)
    weight_term = weight_gradient(level_one, delta_shifts(delta_two)) * scale
    flat_size = weight_term.size
    lanes = 128 if flat_size % 128 == 0 else flat_size
    weight_grad = butterfly_sum(
        weight_term.reshape(flat_size // lanes, lanes), ("depth", "sample")
    ).reshape(weight_term.shape)
    back_part = back_product(shifts_ext, second_kernel)
    act_grad = near_first_scatter(back_part, "height").astype(jnp.bfloat16)
    return (pooled_two, weight_grad, act_grad)


def solution(mesh):
    in_specs = (
        P("sample", None, "depth", "height", None),
        P(),
        P("height", None),
        P("sample", "height", "depth", None),
    )
    out_specs = (
        P("sample", "height", "depth", None),
        P("height", None),
        P("sample", None, "depth", "height", None),
    )
    return jax.shard_map(shards, mesh=mesh, in_specs=in_specs, out_specs=out_specs, check_vma=False)
```

```python
import jax
import jax.numpy as jnp
from jax import lax
from jax.sharding import PartitionSpec as P

LEAK_SLOPE = 0.3
CONV_DIMS = ("NCDHW", "OIDHW", "NCDHW")


def extended(block, sides, width):
    for axis, dim in sides:
        count = lax.axis_size(axis)
        forward = [(i, i + 1) for i in range(count - 1)]
        backward = [(target, source) for source, target in forward]
        low = lax.ppermute(
            lax.slice_in_dim(block, block.shape[dim] - width, None, axis=dim), axis, forward
        )
        high = lax.ppermute(lax.slice_in_dim(block, 0, width, axis=dim), axis, backward)
        block = jnp.concatenate([low, block, high], axis=dim)
    return block


def butterfly_sum(values, axes):
    sizes = [lax.axis_size(axis) for axis in axes]
    count = 1
    for size in sizes:
        count *= size
    if count & (count - 1):
        return lax.psum(values, axes)
    inner = lax.axis_size(axes[-1])

    def label(i):
        low = i % inner
        i = i - low + (low ^ (low >> 1))
        mid = (i // (inner * 2)) % 4
        return i + (((mid ^ (mid >> 1)) - mid) * inner * 2)

    owner = {label(i): i for i in range(count)}
    step = 1
    while step < count:
        pairs = [(i, owner[label(i) ^ step]) for i in range(count)]
        values = values + lax.ppermute(values, axes, pairs)
        step *= 2
    return values


def halving_scatter(values, axis, dim):
    count = lax.axis_size(axis)
    if count & (count - 1):
        return lax.psum_scatter(values, axis, scatter_dimension=dim, tiled=True)
    index = lax.axis_index(axis)
    step = count // 2
    while step >= 1:
        half = values.shape[dim] // 2
        bit = (index // step) % 2
        keep = lax.dynamic_slice_in_dim(values, bit * half, half, axis=dim)
        send = lax.dynamic_slice_in_dim(values, (1 - bit) * half, half, axis=dim)
        pairs = [(i, i ^ step) for i in range(count)]
        values = keep + lax.ppermute(send, axis, pairs)
        step //= 2
    return values


def delta_shifts(delta_ext):
    _, _, _, hsize, wsize = delta_ext.shape
    dpad = jnp.pad(delta_ext[0], ((0, 0), (0, 0), (1, 1), (1, 1)))
    return jnp.stack(
        [
            dpad[:, :, 2 - kh : 2 - kh + hsize, 2 - kw : 2 - kw + wsize]
            for kh in range(3)
            for kw in range(3)
        ],
        axis=1,
    )


def weight_gradient(level_ext, shifted):
    chans = level_ext.shape[1]
    filters, _, dsize, _, _ = shifted.shape
    levels = jnp.stack([level_ext[0, :, kd : kd + dsize] for kd in range(3)], axis=0)
    grad = lax.dot_general(
        shifted,
        levels,
        (((2, 3, 4), (2, 3, 4)), ((), ())),
        preferred_element_type=jnp.float32,
    )
    grad = grad.reshape(filters, 3, 3, 3, chans)
    return jnp.transpose(grad, (0, 4, 3, 1, 2)).reshape(filters, chans * 27)


def back_product(shifts_ext, kernel):
    filters, chans = kernel.shape[:2]
    dsize = shifts_ext.shape[2] - 2
    stacked = jnp.stack(
        [shifts_ext[:, :, 2 - kd : 2 - kd + dsize] for kd in range(3)], axis=0
    )
    weights = jnp.transpose(kernel, (1, 2, 0, 3, 4)).reshape(chans, 3, filters, 9)
    grad = lax.dot_general(
        weights,
        stacked,
        (((1, 2, 3), (0, 1, 2)), ((), ())),
        preferred_element_type=jnp.float32,
    )
    return grad[None]


def forward_product(level_ext, kernel):
    filters, chans = kernel.shape[:2]
    dsize = level_ext.shape[2] - 2
    shifts = delta_shifts(level_ext)
    stacked = jnp.stack([shifts[:, :, kd : kd + dsize] for kd in range(3)], axis=0)
    flipped = jnp.flip(kernel, axis=(3, 4))
    weights = jnp.transpose(flipped, (0, 2, 1, 3, 4)).reshape(filters, 3, chans, 9)
    grad = lax.dot_general(
        weights,
        stacked,
        (((1, 2, 3), (0, 1, 2)), ((), ())),
        preferred_element_type=jnp.float32,
    )
    return grad[None]


def near_first_scatter(values, axis):
    count = lax.axis_size(axis)
    chans, dsize, hsize, wsize = values.shape[1:]
    if count & (count - 1):
        return lax.psum_scatter(values, axis, scatter_dimension=3, tiled=True)
    bits = count.bit_length() - 1
    rows = hsize // count
    index = lax.axis_index(axis)
    grid = jnp.transpose(values[0], (2, 1, 0, 3))
    grid = grid.reshape((2,) * bits + (rows, dsize, chans, wsize))
    for t in range(bits):
        axis_pos = bits - 1 - t
        bit = (index >> t) & 1
        keep = lax.dynamic_slice_in_dim(grid, bit, 1, axis=axis_pos)
        send = lax.dynamic_slice_in_dim(grid, 1 - bit, 1, axis=axis_pos)
        pairs = [(i, i ^ (1 << t)) for i in range(count)]
        grid = jnp.squeeze(keep + lax.ppermute(send, axis, pairs), axis_pos)
    return jnp.transpose(grid, (2, 1, 0, 3))[None]


def activate(values):
    return LEAK_SLOPE * values + (1.0 - LEAK_SLOPE) * jax.nn.softplus(values)


def slope_at(values):
    return LEAK_SLOPE + (1.0 - LEAK_SLOPE) * jax.nn.sigmoid(values)


def pooled(values):
    count, chans, dsize, hsize, wsize = values.shape
    blocks = values.reshape(count, chans, dsize // 2, 2, hsize // 2, 2, wsize // 2, 2)
    return blocks.mean(axis=(3, 5, 7))


def spread_up(values):
    values = jnp.repeat(jnp.repeat(jnp.repeat(values, 2, axis=2), 2, axis=3), 2, axis=4)
    return values * 0.125


def conv_valid(inputs, kernel):
    return lax.conv_general_dilated(
        inputs,
        kernel,
        (1, 1, 1),
        "VALID",
        dimension_numbers=CONV_DIMS,
        preferred_element_type=jnp.float32,
    )


def back_conv(delta_pad, kernel):
    flipped = jnp.flip(kernel, axis=(2, 3, 4))
    return lax.conv_general_dilated(
        delta_pad,
        flipped,
        (1, 1, 1),
        "VALID",
        dimension_numbers=("NCDHW", "IODHW", "NCDHW"),
        preferred_element_type=jnp.float32,
    )


def shards(volume, kernel_one, kernel_two, cotangent):
    depth_count = lax.axis_size("depth")
    height_count = lax.axis_size("height")
    sample_count = lax.axis_size("sample")
    chans_in = volume.shape[1]
    depth_loc = volume.shape[2]
    height_loc = volume.shape[3]
    width_all = volume.shape[4]
    chans_mid = kernel_one.shape[0]
    filters = kernel_two.shape[0]
    first_kernel = kernel_one.reshape(chans_mid, chans_in, 3, 3, 3)
    second_kernel = kernel_two.reshape(filters, chans_mid, 3, 3, 3)
    padded = extended(volume, (("depth", 2), ("height", 3)), 1)
    pre_one = forward_product(padded, first_kernel)[:, :, :, 1:-1]
    level_loc = pooled(activate(pre_one)).astype(jnp.bfloat16)
    slab_rows = lax.all_gather(level_loc, "height", axis=3, tiled=True)
    level_one = extended(slab_rows, (("depth", 2),), 1)
    pre_two = forward_product(level_one, second_kernel)
    pooled_grid = pooled(activate(pre_two)).astype(jnp.bfloat16)
    depth_two = pooled_grid.shape[2]
    pooled_two = pooled_grid.reshape(
        1, filters, depth_two, pooled_grid.shape[3] * pooled_grid.shape[4]
    )
    cot_grid = cotangent.reshape(1, filters, depth_two, pooled_grid.shape[3], pooled_grid.shape[4])
    delta_two = (spread_up(cot_grid.astype(jnp.float32)) * slope_at(pre_two)).astype(jnp.bfloat16)
    scale = 1.0 / float(
        sample_count
        * (depth_loc // 2)
        * depth_count
        * (height_loc // 2)
        * height_count
        * (width_all // 2)
    ) ** 0.5
    delta_ext = extended(delta_two, (("depth", 2),), 1)
    shifts_ext = delta_shifts(delta_ext)
    weight_term = weight_gradient(level_one, delta_shifts(delta_two)) * scale
    flat_size = weight_term.size
    lanes = 128 if flat_size % 128 == 0 else flat_size
    weight_grad = butterfly_sum(
        weight_term.reshape(flat_size // lanes, lanes), ("depth", "sample")
    ).reshape(weight_term.shape)
    back_part = back_product(shifts_ext, second_kernel)
    act_grad = near_first_scatter(back_part, "height").astype(jnp.bfloat16)
    return (pooled_two, weight_grad, act_grad)


def solution(mesh):
    in_specs = (
        P("sample", None, "depth", "height", None),
        P(),
        P("height", None),
        P("sample", "height", "depth", None),
    )
    out_specs = (
        P("sample", "height", "depth", None),
        P("height", None),
        P("sample", None, "depth", "height", None),
    )
    return jax.shard_map(shards, mesh=mesh, in_specs=in_specs, out_specs=out_specs, check_vma=False)
```
